32 devices in a mesh: ctx: 8 (over z, y), roll: 4 (over x, core).
Axes of the slice: x: 2, y: 2, z: 4, core: 2. Of those that a mesh axis runs over, the one named last changes fastest.
Arguments:
- block_order: int32 [8], replicated, may hold values from 0 to 7, as said below
- segment_ids: int32 [1024], replicated, may hold values from 0 to 3, as said below
- layer_input: bfloat16 [8192, 1024], P(None, 'ctx'), may hold values from -6 to 6
- query_states: bfloat16 [1024, 768], P('ctx')
- key_states: bfloat16 [1024, 128], P('ctx')
- value_states: bfloat16 [1024, 128], P('ctx'), may hold values from -6 to 6
- out_grad: bfloat16 [1024, 768], P('ctx'), may hold values from -24 to 24
- master_weight: float32 [8192, 128], P(('ctx', 'roll')), may hold values from -0.0625 to 0.0625
- first_moment: float32 [8192, 128], P(('ctx', 'roll')), may hold values from -60 to 60
- second_moment: float32 [8192, 128], P(('ctx', 'roll')), may hold values from 30 to 3000
Outputs:
- query_grad: bfloat16 [1024, 768], P('ctx')
- key_value_grad: bfloat16 [1024, 256], P('ctx')
- updated_master: float32 [8192, 128], P(('ctx', 'roll'))
- updated_first: float32 [8192, 128], P(('ctx', 'roll'))
- updated_second: float32 [8192, 128], P(('ctx', 'roll'))
- rollout_weight: bfloat16 [8192, 128], P('ctx')
The draws below stay inside these ranges and needn't reach their ends.
Inputs may be any that keep to these rules, and one draw needn't show every extreme that they name: A permutation: index c of ctx holds the tokens at positions block_order[c] * 128 to block_order[c] * 128 + 127, in order; every block is held once. `segment_ids`: ids never fall along sequence positions; there are exactly 4 rollouts; no rollout begins at offset 128 // 2 of a block.
All inputs are finite; a program needn't handle non-finite values.
Results may differ from the reference program's by a relative error of at most 0.028.
Values may be sent and summed in bfloat16 or wider, within the bound.
No kernel may reach another device: no remote copies, remote signals or barrier semaphores. Data moves between devices by JAX's collectives and lax.ppermute only.
A program may use at most 64 MiB of HBM per device.

```python
import math
import jax
import jax.numpy as jnp
from jax import lax

D = 8192
HD = 128
GROUP = 6
NSEG = 4
ROWS = 128
SEQ = 1024
N_CTX = 8


def plan_order(key):
    return jax.random.permutation(jax.random.fold_in(key, 11), N_CTX).astype(jnp.int32)


def draw_block_order(key, part):
    return plan_order(key)


def draw_segment_ids(key, part):
    block_seq = plan_order(key)
    blocks = jax.random.permutation(jax.random.fold_in(key, 12), N_CTX)[:NSEG - 1].astype(jnp.int32)
    offsets = jax.random.randint(jax.random.fold_in(key, 13), (NSEG - 1,), 1, ROWS, dtype=jnp.int32)
    offsets = jnp.where(offsets == ROWS // 2, ROWS // 2 + 1, offsets)
    starts = blocks * ROWS + offsets
    cut_flags = jnp.zeros((SEQ,), jnp.int32).at[starts].set(1)
    in_order = jnp.cumsum(cut_flags).astype(jnp.int32)
    row_positions = (block_seq[:, None] * ROWS + jnp.arange(ROWS, dtype=jnp.int32)[None, :]).reshape(-1)
    return in_order[row_positions]


def draw_key_states(key, part):
    sample = jnp.clip(jax.random.normal(jax.random.fold_in(key, 41), (SEQ, HD), jnp.float32), -5.0, 5.0)
    return sample.astype(jnp.bfloat16)


def draw_query_states(key, part):
    sample = jnp.clip(jax.random.normal(jax.random.fold_in(key, 51), (SEQ, GROUP * HD), jnp.float32), -5.0, 5.0)
    return sample.astype(jnp.bfloat16)


def raised(values, rng, source, target, parts, factor):
    owner, partner = [(jnp.arange(values.shape[dim]) // (values.shape[dim] // parts)).reshape([-1 if axis == dim else 1 for axis in range(values.ndim)]) for dim in (source, target)]
    chosen = jax.random.permutation(rng, parts)[partner]
    strong = (owner == chosen) | (owner == (partner + parts // 2) % parts)
    return jnp.where(strong, factor * values, values)


def block_levels(own_key, extent, cuts, smallest, high):
    level, own = 1.0, jax.random.fold_in(own_key, 6)
    for position, shards_of in cuts:
        steps = jnp.exp(jax.random.uniform(jax.random.fold_in(own, position), (shards_of,), jnp.float32, smallest / len(cuts), high / len(cuts)))
        level = level * jnp.repeat(steps, extent[position] // shards_of).reshape([-1 if axis == position else 1 for axis in range(len(extent))])
    return level


def gaussian(own_key, extent, scale, limit, split=(), kind=jnp.bfloat16):
    result = scale * jax.random.normal(own_key, extent, jnp.float32)
    if split:
        result = result * block_levels(own_key, extent, split, -0.22, 0.18)
    return jnp.clip(result, -limit, limit).astype(kind)


def heavy_noise(stream_key, dims, deviation, most, shards, heavy, held_as=jnp.bfloat16):
    values = deviation * jax.random.normal(stream_key, dims, jnp.float32)
    if shards:
        values = values * block_levels(stream_key, dims, shards, -0.22, 0.18)
    return jnp.clip(raised(values, jax.random.fold_in(stream_key, 3), *heavy), -most, most).astype(held_as)


def setup_inputs(seed: int = 0) -> dict:
    splits = jax.random.split(jax.random.key(seed), 11)
    return {
        "block_order": draw_block_order(jax.random.fold_in(splits[10], 71), 0),
        "segment_ids": draw_segment_ids(jax.random.fold_in(splits[10], 71), 0),
        "layer_input": heavy_noise(splits[2], (D, SEQ), 1.0, 6.0, ((1, 8),), (1, 0, 8, 2.0)),
        "query_states": draw_query_states(jax.random.fold_in(splits[10], 71), 0),
        "key_states": draw_key_states(jax.random.fold_in(splits[10], 71), 0),
        "value_states": gaussian(splits[5], (SEQ, HD), 1.0, 6.0, ((0, 8),)),
        "out_grad": gaussian(splits[6], (SEQ, GROUP * HD), 4.0, 24.0, ((0, 8),)),
        "master_weight": gaussian(splits[7], (D, HD), D ** -0.5, 0.0625, ((0, 32),), jnp.float32),
        "first_moment": gaussian(splits[8], (D, HD), 10.0, 60.0, ((0, 32),), jnp.float32),
        "second_moment": jnp.clip(jnp.exp(math.log(3000.0) - 4.6051702 * jax.random.uniform(splits[9], (D, HD), jnp.float32) ** block_levels(splits[9], (D, HD), ((0, 32),), -0.2, 0.2)), 30.0, 3000.0),
    }


NEG_FILL = -1e+30
BETA_ONE = 0.9
BETA_TWO = 0.95
ADAM_EPS = 1e-08
DECAY_RATE = 0.1
LEARN_RATE = 1e-06
CORRECT_ONE = 0.9999734386011124
CORRECT_TWO = 0.994079470779666

def reference(block_order, segment_ids, layer_input, query_states, key_states, value_states, out_grad, master_weight, first_moment, second_moment):
    score_scale = HD ** (-0.5)
    offsets = jnp.arange(ROWS, dtype=jnp.int32)
    positions = (block_order[:, None] * ROWS + offsets[None, :]).reshape(-1)
    query_blocks = query_states.reshape(N_CTX, ROWS * GROUP, HD)
    grad_blocks = out_grad.reshape(N_CTX, ROWS * GROUP, HD)
    pos_blocks = positions.reshape(N_CTX, ROWS)
    seg_blocks = segment_ids.reshape(N_CTX, ROWS)

    def one_block(carry, inputs):
        q_rows, do_rows, q_pos, q_seg = inputs
        visible = (positions[None, :] <= q_pos[:, None]) & (segment_ids[None, :] == q_seg[:, None])
        visible = jnp.repeat(visible, GROUP, axis=0)
        scores = jnp.dot(q_rows, key_states.T, preferred_element_type=jnp.float32) * score_scale
        scores = jnp.where(visible, scores, NEG_FILL)
        row_top = lax.optimization_barrier(jnp.max(scores, axis=1, keepdims=True))
        expo = jnp.where(visible, jnp.exp(scores - row_top), 0.0)
        log_total = row_top + jnp.log(lax.optimization_barrier(jnp.sum(expo, axis=1, keepdims=True)))
        weights = jnp.where(visible, jnp.exp(scores - log_total), 0.0)
        dprob = jnp.dot(do_rows, value_states.T, preferred_element_type=jnp.float32)
        delta = lax.optimization_barrier(jnp.sum(weights * dprob, axis=1, keepdims=True))
        dscore = weights * (dprob - delta)
        weights_half = weights.astype(jnp.bfloat16)
        dscore_half = dscore.astype(jnp.bfloat16)
        query_part = jnp.dot(dscore_half, key_states, preferred_element_type=jnp.float32) * score_scale
        key_part = jnp.dot(dscore_half.T, q_rows, preferred_element_type=jnp.float32) * score_scale
        value_part = jnp.dot(weights_half.T, do_rows, preferred_element_type=jnp.float32)
        part_half = lax.optimization_barrier(jnp.concatenate([key_part, value_part], axis=1).astype(jnp.bfloat16))
        return (carry + part_half.astype(jnp.float32), query_part.astype(jnp.bfloat16))
    kv_sum, query_parts = lax.scan(one_block, jnp.zeros((SEQ, 2 * HD), jnp.float32), (query_blocks, grad_blocks, pos_blocks, seg_blocks))
    query_grad = query_parts.reshape(SEQ, GROUP * HD)
    key_value_grad = kv_sum.astype(jnp.bfloat16)
    input_blocks = layer_input.reshape(D, N_CTX, ROWS).transpose(1, 0, 2)
    grad_rows = key_value_grad[:, :HD].reshape(N_CTX, ROWS, HD)

    def weight_block(carry, inputs):
        x_block, g_block = inputs
        part = lax.optimization_barrier(jnp.dot(x_block, g_block, preferred_element_type=jnp.float32).astype(jnp.bfloat16))
        return (carry + part.astype(jnp.float32), 0.0)
    weight_grad, unused = lax.scan(weight_block, jnp.zeros((D, HD), jnp.float32), (input_blocks, grad_rows))
    updated_first = BETA_ONE * first_moment + (1.0 - BETA_ONE) * weight_grad
    updated_second = BETA_TWO * second_moment + (1.0 - BETA_TWO) * weight_grad * weight_grad
    update = updated_first / CORRECT_ONE / (jnp.sqrt(updated_second / CORRECT_TWO) + ADAM_EPS) + DECAY_RATE * master_weight
    updated_master = master_weight - LEARN_RATE * update
    rollout_weight = updated_master.astype(jnp.bfloat16)
    return (query_grad, key_value_grad, updated_master, updated_first, updated_second, rollout_weight)
```

```python
import jax
import jax.numpy as jnp
from jax import lax
from jax.sharding import PartitionSpec as P

NEG_FILL = -1e30
BETA_ONE = 0.9
BETA_TWO = 0.95
ADAM_EPS = 1e-08
DECAY_RATE = 0.1
LEARN_RATE = 1e-06
CORRECT_ONE = 0.9999734386011124
CORRECT_TWO = 0.994079470779666


def shifted(value, axis, count, shift):
    return lax.ppermute(value, axis, [(i, (i + shift) % count) for i in range(count)])


def body(
    block_order,
    segment_ids,
    layer_input,
    query_states,
    key_states,
    value_states,
    out_grad,
    master_weight,
    first_moment,
    second_moment,
):
    row_count, head_dim = key_states.shape
    head_group = query_states.shape[1] // head_dim
    ctx_count = lax.axis_size("ctx")
    roll_count = lax.axis_size("roll")
    ctx_rank = lax.axis_index("ctx")
    roll_rank = lax.axis_index("roll")
    score_scale = head_dim ** (-0.5)

    offsets = jnp.arange(row_count, dtype=jnp.int32)
    pos_table = block_order[:, None] * row_count + offsets[None, :]
    seg_table = segment_ids.reshape(ctx_count, row_count)
    q_pos = lax.dynamic_index_in_dim(pos_table, ctx_rank, 0, keepdims=False)
    q_seg = lax.dynamic_index_in_dim(seg_table, ctx_rank, 0, keepdims=False)

    own_kv = jnp.concatenate([key_states, value_states], axis=1)
    kv_blocks = [own_kv] + [
        shifted(own_kv, "ctx", ctx_count, s) for s in range(1, ctx_count)
    ]
    kv_all = jnp.concatenate(kv_blocks, axis=0)
    key_all = kv_all[:, :head_dim]
    value_all = kv_all[:, head_dim:]
    sources = (ctx_rank - jnp.arange(ctx_count, dtype=jnp.int32)) % ctx_count
    key_pos = jnp.take(pos_table, sources, axis=0).reshape(-1)
    key_seg = jnp.take(seg_table, sources, axis=0).reshape(-1)

    q_rows = query_states.reshape(row_count * head_group, head_dim)
    do_rows = out_grad.reshape(row_count * head_group, head_dim)
    visible = (key_pos[None, :] <= q_pos[:, None]) & (key_seg[None, :] == q_seg[:, None])
    visible = jnp.repeat(visible, head_group, axis=0)
    scores = jnp.dot(q_rows, key_all.T, preferred_element_type=jnp.float32) * score_scale
    scores = jnp.where(visible, scores, NEG_FILL)
    row_top = jnp.max(scores, axis=1, keepdims=True)
    expo = jnp.where(visible, jnp.exp(scores - row_top), 0.0)
    log_total = row_top + jnp.log(jnp.sum(expo, axis=1, keepdims=True))
    weights = jnp.where(visible, jnp.exp(scores - log_total), 0.0)
    dprob = jnp.dot(do_rows, value_all.T, preferred_element_type=jnp.float32)
    delta = jnp.sum(weights * dprob, axis=1, keepdims=True)
    dscore = weights * (dprob - delta)
    weights_half = weights.astype(jnp.bfloat16)
    dscore_half = dscore.astype(jnp.bfloat16)
    query_part = jnp.dot(dscore_half, key_all, preferred_element_type=jnp.float32) * score_scale
    query_grad = query_part.astype(jnp.bfloat16).reshape(row_count, head_group * head_dim)
    key_part = jnp.dot(dscore_half.T, q_rows, preferred_element_type=jnp.float32) * score_scale
    value_part = jnp.dot(weights_half.T, do_rows, preferred_element_type=jnp.float32)
    part_half = jnp.concatenate([key_part, value_part], axis=1).astype(jnp.bfloat16)
    part_blocks = part_half.reshape(ctx_count, row_count, 2 * head_dim)

    kv_sum = part_blocks[0].astype(jnp.float32)
    for s in range(1, ctx_count):
        kv_sum = kv_sum + shifted(part_blocks[s], "ctx", ctx_count, -s).astype(jnp.float32)
    key_value = kv_sum.astype(jnp.bfloat16)
    key_grad = key_value[:, :head_dim]

    owner_rows = master_weight.shape[0]
    picked = lax.dynamic_index_in_dim(
        layer_input.reshape(ctx_count, roll_count, owner_rows, row_count),
        roll_rank,
        1,
        keepdims=False,
    )
    products = jnp.einsum(
        "csr,rh->csh", picked, key_grad, preferred_element_type=jnp.float32
    ).astype(jnp.bfloat16)
    weight_grad = lax.dynamic_index_in_dim(products, ctx_rank, 0, keepdims=False).astype(
        jnp.float32
    )
    for s in range(1, ctx_count):
        outgoing = lax.dynamic_index_in_dim(
            products, (ctx_rank + s) % ctx_count, 0, keepdims=False
        )
        weight_grad = weight_grad + shifted(outgoing, "ctx", ctx_count, s).astype(jnp.float32)

    updated_first = BETA_ONE * first_moment + (1.0 - BETA_ONE) * weight_grad
    updated_second = BETA_TWO * second_moment + (1.0 - BETA_TWO) * weight_grad * weight_grad
    update = (
        updated_first / CORRECT_ONE / (jnp.sqrt(updated_second / CORRECT_TWO) + ADAM_EPS)
        + DECAY_RATE * master_weight
    )
    updated_master = master_weight - LEARN_RATE * update
    rollout_weight = lax.all_gather(updated_master.astype(jnp.bfloat16), "roll", axis=0, tiled=True)
    return (query_grad, key_value, updated_master, updated_first, updated_second, rollout_weight)


def solution(mesh):
    placed = (
        P(),
        P(),
        P(None, "ctx"),
        P("ctx", None),
        P("ctx", None),
        P("ctx", None),
        P("ctx", None),
        P(("ctx", "roll"), None),
        P(("ctx", "roll"), None),
        P(("ctx", "roll"), None),
    )
    return jax.shard_map(
        body,
        mesh=mesh,
        in_specs=placed,
        out_specs=(
            P("ctx", None),
            P("ctx", None),
            P(("ctx", "roll"), None),
            P(("ctx", "roll"), None),
            P(("ctx", "roll"), None),
            P("ctx", None),
        ),
        check_vma=False,
    )
```

```python
import jax
import jax.numpy as jnp
from jax import lax
from jax.sharding import PartitionSpec as P


NEG_FILL = -1e30
BETA_ONE = 0.9
BETA_TWO = 0.95
ADAM_EPS = 1e-08
DECAY_RATE = 0.1
LEARN_RATE = 1e-06
CORRECT_ONE = 0.9999734386011124
CORRECT_TWO = 0.994079470779666


def shifted(value, axis, count, shift):
    return lax.ppermute(value, axis, [(i, (i + shift) % count) for i in range(count)])


def body(
    block_order,
    segment_ids,
    layer_input,
    query_states,
    key_states,
    value_states,
    out_grad,
    master_weight,
    first_moment,
    second_moment,
):
    row_count, head_dim = key_states.shape
    head_group = query_states.shape[1] // head_dim
    ctx_count = lax.axis_size("ctx")
    roll_count = lax.axis_size("roll")
    ctx_rank = lax.axis_index("ctx")
    roll_rank = lax.axis_index("roll")
    score_scale = head_dim ** (-0.5)

    offsets = jnp.arange(row_count, dtype=jnp.int32)
    pos_table = block_order[:, None] * row_count + offsets[None, :]
    seg_table = segment_ids.reshape(ctx_count, row_count)
    q_pos = lax.dynamic_index_in_dim(pos_table, ctx_rank, 0, keepdims=False)
    q_seg = lax.dynamic_index_in_dim(seg_table, ctx_rank, 0, keepdims=False)

    own_kv = jnp.concatenate([key_states, value_states], axis=1)
    kv_blocks = [own_kv] + [
        shifted(own_kv, "ctx", ctx_count, -s) for s in range(1, ctx_count)
    ]
    kv_all = jnp.concatenate(kv_blocks, axis=0)
    key_all = kv_all[:, :head_dim]
    value_all = kv_all[:, head_dim:]
    pos_twice = jnp.concatenate([pos_table, pos_table], axis=0)
    seg_twice = jnp.concatenate([seg_table, seg_table], axis=0)
    key_pos = lax.dynamic_slice_in_dim(pos_twice, ctx_rank, ctx_count, 0).reshape(-1)
    key_seg = lax.dynamic_slice_in_dim(seg_twice, ctx_rank, ctx_count, 0).reshape(-1)
    key_count = key_pos.shape[0]

    q_rows = query_states.reshape(row_count * head_group, head_dim)
    do_rows = out_grad.reshape(row_count * head_group, head_dim)
    visible = (key_pos[None, :] <= q_pos[:, None]) & (key_seg[None, :] == q_seg[:, None])
    visible = visible[:, None, :]

    def by_token(rows):
        return rows.reshape(row_count, head_group, key_count)

    def by_row(values):
        return values.reshape(row_count * head_group, key_count)

    scores = jnp.dot(q_rows, key_all.T, preferred_element_type=jnp.float32) * score_scale
    scores = jnp.where(visible, by_token(scores), NEG_FILL)
    row_top = jnp.max(scores, axis=2, keepdims=True)
    expo = jnp.where(visible, jnp.exp(scores - row_top), 0.0)
    log_total = row_top + jnp.log(jnp.sum(expo, axis=2, keepdims=True))
    weights = jnp.where(visible, jnp.exp(scores - log_total), 0.0)
    dprob = by_token(jnp.dot(do_rows, value_all.T, preferred_element_type=jnp.float32))
    delta = jnp.sum(weights * dprob, axis=2, keepdims=True)
    dscore = weights * (dprob - delta)
    weights_half = by_row(weights.astype(jnp.bfloat16))
    dscore_half = by_row(dscore.astype(jnp.bfloat16))
    query_part = jnp.dot(dscore_half, key_all, preferred_element_type=jnp.float32) * score_scale
    query_grad = query_part.astype(jnp.bfloat16).reshape(row_count, head_group * head_dim)
    key_part = jnp.dot(dscore_half.T, q_rows, preferred_element_type=jnp.float32) * score_scale
    value_part = jnp.dot(weights_half.T, do_rows, preferred_element_type=jnp.float32)
    part_half = jnp.concatenate([key_part, value_part], axis=1).astype(jnp.bfloat16)
    part_blocks = part_half.reshape(ctx_count, row_count, 2 * head_dim)

    kv_sum = part_blocks[0].astype(jnp.float32)
    for s in range(1, ctx_count):
        kv_sum = kv_sum + shifted(part_blocks[s], "ctx", ctx_count, s).astype(jnp.float32)
    key_value = kv_sum.astype(jnp.bfloat16)
    key_grad = key_value[:, :head_dim]

    owner_rows = master_weight.shape[0]
    picked = lax.dynamic_index_in_dim(
        layer_input.reshape(ctx_count, roll_count, owner_rows, row_count),
        roll_rank,
        1,
        keepdims=False,
    )
    products = jnp.einsum(
        "csr,rh->csh", picked, key_grad, preferred_element_type=jnp.float32
    ).astype(jnp.bfloat16)
    weight_grad = lax.dynamic_index_in_dim(products, ctx_rank, 0, keepdims=False).astype(
        jnp.float32
    )
    for s in range(1, ctx_count):
        outgoing = lax.dynamic_index_in_dim(
            products, (ctx_rank + s) % ctx_count, 0, keepdims=False
        )
        weight_grad = weight_grad + shifted(outgoing, "ctx", ctx_count, s).astype(jnp.float32)

    updated_first = BETA_ONE * first_moment + (1.0 - BETA_ONE) * weight_grad
    updated_second = BETA_TWO * second_moment + (1.0 - BETA_TWO) * weight_grad * weight_grad
    update = (
        updated_first / CORRECT_ONE / (jnp.sqrt(updated_second / CORRECT_TWO) + ADAM_EPS)
        + DECAY_RATE * master_weight
    )
    updated_master = master_weight - LEARN_RATE * update
    rollout_weight = lax.all_gather(updated_master.astype(jnp.bfloat16), "roll", axis=0, tiled=True)
    return (query_grad, key_value, updated_master, updated_first, updated_second, rollout_weight)


def solution(mesh):
    placed = (
        P(),
        P(),
        P(None, "ctx"),
        P("ctx", None),
        P("ctx", None),
        P("ctx", None),
        P("ctx", None),
        P(("ctx", "roll"), None),
        P(("ctx", "roll"), None),
        P(("ctx", "roll"), None),
    )
    return jax.shard_map(
        body,
        mesh=mesh,
        in_specs=placed,
        out_specs=(
            P("ctx", None),
            P("ctx", None),
            P(("ctx", "roll"), None),
            P(("ctx", "roll"), None),
            P(("ctx", "roll"), None),
            P("ctx", None),
        ),
        check_vma=False,
    )
```

```python
import functools

import jax
import jax.numpy as jnp
from jax import lax
from jax.experimental import pallas as pl
from jax.experimental.pallas import tpu as pltpu
from jax.sharding import PartitionSpec as P


NEG_FILL = -1e30
BETA_ONE = 0.9
BETA_TWO = 0.95
ADAM_EPS = 1e-08
DECAY_RATE = 0.1
LEARN_RATE = 1e-06
CORRECT_ONE = 0.9999734386011124
CORRECT_TWO = 0.994079470779666


def shifted(value, axis, count, shift):
    return lax.ppermute(value, axis, [(i, (i + shift) % count) for i in range(count)])


def attention_kernel(block_count, block_rows, head_dim, score_scale, *refs):
    qpos_ref, qseg_ref, kpos_ref, kseg_ref, q_ref, do_ref = refs[:6]
    kv_refs = refs[6 : 6 + block_count]
    dq_ref, part_ref = refs[6 + block_count : 8 + block_count]
    kv_scr, dk_acc, dv_acc = refs[8 + block_count :]
    step = pl.program_id(0)

    @pl.when(step == 0)
    def _():
        for b in range(block_count):
            kv_scr[b * block_rows : (b + 1) * block_rows, :] = kv_refs[b][...]
        dk_acc[...] = jnp.zeros_like(dk_acc)
        dv_acc[...] = jnp.zeros_like(dv_acc)

    q = q_ref[...]
    do = do_ref[...]
    key_all = kv_scr[:, :head_dim]
    value_all = kv_scr[:, head_dim:]
    last_dims = (((1,), (1,)), ((), ()))
    first_dims = (((0,), (0,)), ((), ()))
    visible = (kpos_ref[...] <= qpos_ref[...]) & (kseg_ref[...] == qseg_ref[...])
    scores = lax.dot_general(q, key_all, last_dims, preferred_element_type=jnp.float32) * score_scale
    scores = jnp.where(visible, scores, NEG_FILL)
    row_top = jnp.max(scores, axis=1, keepdims=True)
    expo = jnp.where(visible, jnp.exp(scores - row_top), 0.0)
    log_total = row_top + jnp.log(jnp.sum(expo, axis=1, keepdims=True))
    weights = jnp.where(visible, jnp.exp(scores - log_total), 0.0)
    dprob = lax.dot_general(do, value_all, last_dims, preferred_element_type=jnp.float32)
    delta = jnp.sum(weights * dprob, axis=1, keepdims=True)
    dscore = weights * (dprob - delta)
    weights_half = weights.astype(jnp.bfloat16)
    dscore_half = dscore.astype(jnp.bfloat16)
    query_part = jnp.dot(dscore_half, key_all, preferred_element_type=jnp.float32) * score_scale
    dq_ref[...] = query_part.astype(dq_ref.dtype)
    dk_acc[...] += lax.dot_general(dscore_half, q, first_dims, preferred_element_type=jnp.float32)
    dv_acc[...] += lax.dot_general(weights_half, do, first_dims, preferred_element_type=jnp.float32)

    @pl.when(step == pl.num_programs(0) - 1)
    def _():
        part_ref[:, :head_dim] = (dk_acc[...] * score_scale).astype(part_ref.dtype)
        part_ref[:, head_dim:] = dv_acc[...].astype(part_ref.dtype)


def attention_backward(qpos_rows, qseg_rows, key_pos, key_seg, q_rows, do_rows, kv_blocks, score_scale):
    row_total, head_dim = q_rows.shape
    block_count = len(kv_blocks)
    block_rows = kv_blocks[0].shape[0]
    key_count = block_count * block_rows
    tile = row_total
    while tile * key_count > 384 * 1024 and tile % 16 == 0:
        tile //= 2
    grid = (row_total // tile,)
    full = lambda shape: pl.BlockSpec(shape, lambda i: (0,) * len(shape))
    rows = lambda width: pl.BlockSpec((tile, width), lambda i: (i, 0))
    kernel = functools.partial(attention_kernel, block_count, block_rows, head_dim, score_scale)
    return pl.pallas_call(
        kernel,
        grid=grid,
        in_specs=[rows(1), rows(1), full((1, key_count)), full((1, key_count)), rows(head_dim), rows(head_dim)]
        + [full((block_rows, 2 * head_dim))] * block_count,
        out_specs=[rows(head_dim), full((key_count, 2 * head_dim))],
        out_shape=[
            jax.ShapeDtypeStruct((row_total, head_dim), jnp.bfloat16),
            jax.ShapeDtypeStruct((key_count, 2 * head_dim), jnp.bfloat16),
        ],
        scratch_shapes=[
            pltpu.VMEM((key_count, 2 * head_dim), jnp.bfloat16),
            pltpu.VMEM((key_count, head_dim), jnp.float32),
            pltpu.VMEM((key_count, head_dim), jnp.float32),
        ],
        compiler_params=pltpu.CompilerParams(dimension_semantics=("arbitrary",)),
    )(qpos_rows, qseg_rows, key_pos, key_seg, q_rows, do_rows, *kv_blocks)


def body(
    block_order,
    segment_ids,
    layer_input,
    query_states,
    key_states,
    value_states,
    out_grad,
    master_weight,
    first_moment,
    second_moment,
):
    row_count, head_dim = key_states.shape
    head_group = query_states.shape[1] // head_dim
    ctx_count = lax.axis_size("ctx")
    roll_count = lax.axis_size("roll")
    ctx_rank = lax.axis_index("ctx")
    roll_rank = lax.axis_index("roll")
    score_scale = head_dim ** (-0.5)

    offsets = jnp.arange(row_count, dtype=jnp.int32)
    pos_table = block_order[:, None] * row_count + offsets[None, :]
    seg_table = segment_ids.reshape(ctx_count, row_count)
    q_pos = lax.dynamic_index_in_dim(pos_table, ctx_rank, 0, keepdims=False)
    q_seg = lax.dynamic_index_in_dim(seg_table, ctx_rank, 0, keepdims=False)

    own_kv = jnp.concatenate([key_states, value_states], axis=1)
    kv_blocks = [own_kv] + [
        shifted(own_kv, "ctx", ctx_count, -s) for s in range(1, ctx_count)
    ]
    pos_twice = jnp.concatenate([pos_table, pos_table], axis=0)
    seg_twice = jnp.concatenate([seg_table, seg_table], axis=0)
    key_pos = lax.dynamic_slice_in_dim(pos_twice, ctx_rank, ctx_count, 0).reshape(1, -1)
    key_seg = lax.dynamic_slice_in_dim(seg_twice, ctx_rank, ctx_count, 0).reshape(1, -1)

    q_rows = query_states.reshape(row_count * head_group, head_dim)
    do_rows = out_grad.reshape(row_count * head_group, head_dim)
    qpos_rows = jnp.repeat(q_pos, head_group)[:, None]
    qseg_rows = jnp.repeat(q_seg, head_group)[:, None]
    query_part, part_half = attention_backward(
        qpos_rows, qseg_rows, key_pos, key_seg, q_rows, do_rows, kv_blocks, score_scale
    )
    query_grad = query_part.reshape(row_count, head_group * head_dim)
    part_blocks = part_half.reshape(ctx_count, row_count, 2 * head_dim)

    kv_sum = part_blocks[0].astype(jnp.float32)
    for s in range(1, ctx_count):
        kv_sum = kv_sum + shifted(part_blocks[s], "ctx", ctx_count, s).astype(jnp.float32)
    key_value = kv_sum.astype(jnp.bfloat16)
    key_grad = key_value[:, :head_dim]

    owner_rows = master_weight.shape[0]
    picked = lax.dynamic_index_in_dim(
        layer_input.reshape(ctx_count, roll_count, owner_rows, row_count),
        roll_rank,
        1,
        keepdims=False,
    )
    products = jnp.einsum(
        "csr,rh->csh", picked, key_grad, preferred_element_type=jnp.float32
    ).astype(jnp.bfloat16)
    weight_grad = lax.dynamic_index_in_dim(products, ctx_rank, 0, keepdims=False).astype(
        jnp.float32
    )
    for s in range(1, ctx_count):
        outgoing = lax.dynamic_index_in_dim(
            products, (ctx_rank + s) % ctx_count, 0, keepdims=False
        )
        weight_grad = weight_grad + shifted(outgoing, "ctx", ctx_count, s).astype(jnp.float32)

    updated_first = BETA_ONE * first_moment + (1.0 - BETA_ONE) * weight_grad
    updated_second = BETA_TWO * second_moment + (1.0 - BETA_TWO) * weight_grad * weight_grad
    update = (
        updated_first / CORRECT_ONE / (jnp.sqrt(updated_second / CORRECT_TWO) + ADAM_EPS)
        + DECAY_RATE * master_weight
    )
    updated_master = master_weight - LEARN_RATE * update
    rollout_weight = lax.all_gather(updated_master.astype(jnp.bfloat16), "roll", axis=0, tiled=True)
    return (query_grad, key_value, updated_master, updated_first, updated_second, rollout_weight)


def solution(mesh):
    placed = (
        P(),
        P(),
        P(None, "ctx"),
        P("ctx", None),
        P("ctx", None),
        P("ctx", None),
        P("ctx", None),
        P(("ctx", "roll"), None),
        P(("ctx", "roll"), None),
        P(("ctx", "roll"), None),
    )
    return jax.shard_map(
        body,
        mesh=mesh,
        in_specs=placed,
        out_specs=(
            P("ctx", None),
            P("ctx", None),
            P(("ctx", "roll"), None),
            P(("ctx", "roll"), None),
            P(("ctx", "roll"), None),
            P("ctx", None),
        ),
        check_vma=False,
    )
```

```python
import functools

import jax
import jax.numpy as jnp
from jax import lax
from jax.experimental import pallas as pl
from jax.experimental.pallas import tpu as pltpu
from jax.sharding import PartitionSpec as P


NEG_FILL = -1e30
BETA_ONE = 0.9
BETA_TWO = 0.95
ADAM_EPS = 1e-08
DECAY_RATE = 0.1
LEARN_RATE = 1e-06
CORRECT_ONE = 0.9999734386011124
CORRECT_TWO = 0.994079470779666


def shifted(value, axis, count, shift):
    return lax.ppermute(value, axis, [(i, (i + shift) % count) for i in range(count)])


def attention_kernel(block_count, block_rows, head_dim, score_scale, *refs):
    qpos_ref, qseg_ref, kpos_ref, kseg_ref, q_ref, do_ref = refs[:6]
    kv_refs = refs[6 : 6 + block_count]
    dq_ref, part_ref = refs[6 + block_count : 8 + block_count]
    kv_scr, dk_acc, dv_acc = refs[8 + block_count :]
    step = pl.program_id(0)

    @pl.when(step == 0)
    def _():
        for b in range(block_count):
            kv_scr[b * block_rows : (b + 1) * block_rows, :] = kv_refs[b][...]
        dk_acc[...] = jnp.zeros_like(dk_acc)
        dv_acc[...] = jnp.zeros_like(dv_acc)

    q = q_ref[...]
    do = do_ref[...]
    key_all = kv_scr[:, :head_dim]
    value_all = kv_scr[:, head_dim:]
    last_dims = (((1,), (1,)), ((), ()))
    first_dims = (((0,), (0,)), ((), ()))
    visible = (kpos_ref[...] <= qpos_ref[...]) & (kseg_ref[...] == qseg_ref[...])
    scores = lax.dot_general(q, key_all, last_dims, preferred_element_type=jnp.float32) * score_scale
    scores = jnp.where(visible, scores, NEG_FILL)
    row_top = jnp.max(scores, axis=1, keepdims=True)
    expo = jnp.where(visible, jnp.exp(scores - row_top), 0.0)
    weights = expo * (1.0 / jnp.sum(expo, axis=1, keepdims=True))
    dprob = lax.dot_general(do, value_all, last_dims, preferred_element_type=jnp.float32)
    delta = jnp.sum(weights * dprob, axis=1, keepdims=True)
    dscore = weights * (dprob - delta)
    weights_half = weights.astype(jnp.bfloat16)
    dscore_half = dscore.astype(jnp.bfloat16)
    query_part = jnp.dot(dscore_half, key_all, preferred_element_type=jnp.float32) * score_scale
    dq_ref[...] = query_part.astype(dq_ref.dtype)
    dk_acc[...] += lax.dot_general(dscore_half, q, first_dims, preferred_element_type=jnp.float32)
    dv_acc[...] += lax.dot_general(weights_half, do, first_dims, preferred_element_type=jnp.float32)

    @pl.when(step == pl.num_programs(0) - 1)
    def _():
        for b in range(block_count):
            rows = slice(b * block_rows, (b + 1) * block_rows)
            part_ref[b, :, :head_dim] = (dk_acc[rows, :] * score_scale).astype(part_ref.dtype)
            part_ref[b, :, head_dim:] = dv_acc[rows, :].astype(part_ref.dtype)


def attention_backward(q_pos, q_seg, key_pos, key_seg, query_states, out_grad, kv_blocks, head_dim, score_scale):
    row_count, width = query_states.shape
    head_group = width // head_dim
    block_count = len(kv_blocks)
    block_rows = kv_blocks[0].shape[0]
    key_count = block_count * block_rows
    full = lambda shape: pl.BlockSpec(shape, lambda h: (0,) * len(shape))
    head = pl.BlockSpec((row_count, head_dim), lambda h: (0, h))
    kernel = functools.partial(attention_kernel, block_count, block_rows, head_dim, score_scale)
    return pl.pallas_call(
        kernel,
        grid=(head_group,),
        in_specs=[full((row_count, 1)), full((row_count, 1)), full((1, key_count)), full((1, key_count)), head, head]
        + [full((block_rows, 2 * head_dim))] * block_count,
        out_specs=[head, full((block_count, block_rows, 2 * head_dim))],
        out_shape=[
            jax.ShapeDtypeStruct((row_count, width), jnp.bfloat16),
            jax.ShapeDtypeStruct((block_count, block_rows, 2 * head_dim), jnp.bfloat16),
        ],
        scratch_shapes=[
            pltpu.VMEM((key_count, 2 * head_dim), jnp.bfloat16),
            pltpu.VMEM((key_count, head_dim), jnp.float32),
            pltpu.VMEM((key_count, head_dim), jnp.float32),
        ],
        compiler_params=pltpu.CompilerParams(dimension_semantics=("arbitrary",)),
    )(q_pos[:, None], q_seg[:, None], key_pos, key_seg, query_states, out_grad, *kv_blocks)


def body(
    block_order,
    segment_ids,
    layer_input,
    query_states,
    key_states,
    value_states,
    out_grad,
    master_weight,
    first_moment,
    second_moment,
):
    row_count, head_dim = key_states.shape
    head_group = query_states.shape[1] // head_dim
    ctx_count = lax.axis_size("ctx")
    roll_count = lax.axis_size("roll")
    ctx_rank = lax.axis_index("ctx")
    roll_rank = lax.axis_index("roll")
    score_scale = head_dim ** (-0.5)

    offsets = jnp.arange(row_count, dtype=jnp.int32)
    pos_table = block_order[:, None] * row_count + offsets[None, :]
    seg_table = segment_ids.reshape(ctx_count, row_count)
    q_pos = lax.dynamic_index_in_dim(pos_table, ctx_rank, 0, keepdims=False)
    q_seg = lax.dynamic_index_in_dim(seg_table, ctx_rank, 0, keepdims=False)

    own_kv = jnp.concatenate([key_states, value_states], axis=1)
    kv_blocks = [own_kv] + [
        shifted(own_kv, "ctx", ctx_count, -s) for s in range(1, ctx_count)
    ]
    pos_twice = jnp.concatenate([pos_table, pos_table], axis=0)
    seg_twice = jnp.concatenate([seg_table, seg_table], axis=0)
    key_pos = lax.dynamic_slice_in_dim(pos_twice, ctx_rank, ctx_count, 0).reshape(1, -1)
    key_seg = lax.dynamic_slice_in_dim(seg_twice, ctx_rank, ctx_count, 0).reshape(1, -1)

    query_grad, part_blocks = attention_backward(
        q_pos, q_seg, key_pos, key_seg, query_states, out_grad, kv_blocks, head_dim, score_scale
    )

    kv_sum = part_blocks[0].astype(jnp.float32)
    for s in range(1, ctx_count):
        kv_sum = kv_sum + shifted(part_blocks[s], "ctx", ctx_count, s).astype(jnp.float32)
    key_value = kv_sum.astype(jnp.bfloat16)
    key_grad = key_value[:, :head_dim]

    owner_rows = master_weight.shape[0]
    picked = lax.dynamic_index_in_dim(
        layer_input.reshape(ctx_count, roll_count, owner_rows, row_count),
        roll_rank,
        1,
        keepdims=False,
    )
    products = jnp.einsum(
        "csr,rh->csh", picked, key_grad, preferred_element_type=jnp.float32
    ).astype(jnp.bfloat16)
    weight_grad = lax.dynamic_index_in_dim(products, ctx_rank, 0, keepdims=False).astype(
        jnp.float32
    )
    for s in range(1, ctx_count):
        outgoing = lax.dynamic_index_in_dim(
            products, (ctx_rank + s) % ctx_count, 0, keepdims=False
        )
        weight_grad = weight_grad + shifted(outgoing, "ctx", ctx_count, s).astype(jnp.float32)

    updated_first = BETA_ONE * first_moment + (1.0 - BETA_ONE) * weight_grad
    updated_second = BETA_TWO * second_moment + (1.0 - BETA_TWO) * weight_grad * weight_grad
    update = (
        updated_first / CORRECT_ONE / (jnp.sqrt(updated_second / CORRECT_TWO) + ADAM_EPS)
        + DECAY_RATE * master_weight
    )
    updated_master = master_weight - LEARN_RATE * update
    rollout_weight = lax.all_gather(updated_master.astype(jnp.bfloat16), "roll", axis=0, tiled=True)
    return (query_grad, key_value, updated_master, updated_first, updated_second, rollout_weight)


def solution(mesh):
    placed = (
        P(),
        P(),
        P(None, "ctx"),
        P("ctx", None),
        P("ctx", None),
        P("ctx", None),
        P("ctx", None),
        P(("ctx", "roll"), None),
        P(("ctx", "roll"), None),
        P(("ctx", "roll"), None),
    )
    return jax.shard_map(
        body,
        mesh=mesh,
        in_specs=placed,
        out_specs=(
            P("ctx", None),
            P("ctx", None),
            P(("ctx", "roll"), None),
            P(("ctx", "roll"), None),
            P(("ctx", "roll"), None),
            P("ctx", None),
        ),
        check_vma=False,
    )
```

```python
import functools

import jax
import jax.numpy as jnp
from jax import lax
from jax.experimental import pallas as pl
from jax.experimental.pallas import tpu as pltpu
from jax.sharding import PartitionSpec as P


NEG_FILL = -1e30
BETA_ONE = 0.9
BETA_TWO = 0.95
ADAM_EPS = 1e-08
DECAY_RATE = 0.1
LEARN_RATE = 1e-06
CORRECT_ONE = 0.9999734386011124
CORRECT_TWO = 0.994079470779666


def shifted(value, axis, count, shift):
    return lax.ppermute(value, axis, [(i, (i + shift) % count) for i in range(count)])


def attention_kernel(block_count, block_rows, head_dim, score_scale, *refs):
    order_ref, rank_ref, seg_ref, q_ref, do_ref = refs[:5]
    kv_refs = refs[5 : 5 + block_count]
    dq_ref = refs[5 + block_count]
    part_refs = refs[6 + block_count : 6 + 2 * block_count]
    kv_scr, mask_scr, dk_acc, dv_acc = refs[6 + 2 * block_count :]
    step = pl.program_id(0)

    @pl.when(step == 0)
    def _():
        rank = rank_ref[0]
        lane = lax.broadcasted_iota(jnp.int32, (block_rows, block_rows), 1)
        sub = lax.broadcasted_iota(jnp.int32, (block_rows, block_rows), 0)
        own_seg = seg_ref[pl.ds(rank, 1), :]
        q_seg = jnp.sum(jnp.where(lane == sub, own_seg, 0), axis=1, keepdims=True)
        q_pos = order_ref[rank] * block_rows + sub[:, :1]
        for b in range(block_count):
            source = (rank + b) % block_count
            k_pos = order_ref[source] * block_rows + lane[:1, :]
            k_seg = seg_ref[pl.ds(source, 1), :]
            visible = (k_pos <= q_pos) & (k_seg == q_seg)
            cols = slice(b * block_rows, (b + 1) * block_rows)
            mask_scr[:, cols] = visible.astype(jnp.int32)
            kv_scr[0, cols, :] = kv_refs[b][0]
            kv_scr[1, cols, :] = kv_refs[b][1]
        dk_acc[...] = jnp.zeros_like(dk_acc)
        dv_acc[...] = jnp.zeros_like(dv_acc)

    q = q_ref[...]
    do = do_ref[...]
    key_all = kv_scr[0]
    value_all = kv_scr[1]
    last_dims = (((1,), (1,)), ((), ()))
    first_dims = (((0,), (0,)), ((), ()))
    visible = mask_scr[...] != 0
    scores = lax.dot_general(q, key_all, last_dims, preferred_element_type=jnp.float32) * score_scale
    scores = jnp.where(visible, scores, NEG_FILL)
    row_top = jnp.max(scores, axis=1, keepdims=True)
    expo = jnp.where(visible, jnp.exp(scores - row_top), 0.0)
    weights = expo * (1.0 / jnp.sum(expo, axis=1, keepdims=True))
    dprob = lax.dot_general(do, value_all, last_dims, preferred_element_type=jnp.float32)
    delta = jnp.sum(weights * dprob, axis=1, keepdims=True)
    dscore = weights * (dprob - delta)
    weights_half = weights.astype(jnp.bfloat16)
    dscore_half = dscore.astype(jnp.bfloat16)
    query_part = jnp.dot(dscore_half, key_all, preferred_element_type=jnp.float32) * score_scale
    dq_ref[...] = query_part.astype(dq_ref.dtype)
    dk_acc[...] += lax.dot_general(dscore_half, q, first_dims, preferred_element_type=jnp.float32)
    dv_acc[...] += lax.dot_general(weights_half, do, first_dims, preferred_element_type=jnp.float32)

    @pl.when(step == pl.num_programs(0) - 1)
    def _():
        for b in range(block_count):
            rows = slice(b * block_rows, (b + 1) * block_rows)
            part_refs[b][:, :head_dim] = (dk_acc[rows, :] * score_scale).astype(jnp.bfloat16)
            part_refs[b][:, head_dim:] = dv_acc[rows, :].astype(jnp.bfloat16)


def attention_backward(block_order, rank, seg_rows, query_states, out_grad, kv_blocks, head_dim, score_scale):
    row_count, width = query_states.shape
    head_group = width // head_dim
    block_count = len(kv_blocks)
    block_rows = kv_blocks[0].shape[1]
    key_count = block_count * block_rows
    full = lambda shape: pl.BlockSpec(shape, lambda h, *_: (0,) * len(shape))
    head = pl.BlockSpec((row_count, head_dim), lambda h, *_: (0, h))
    part = jax.ShapeDtypeStruct((block_rows, 2 * head_dim), jnp.bfloat16)
    kernel = functools.partial(attention_kernel, block_count, block_rows, head_dim, score_scale)
    outs = pl.pallas_call(
        kernel,
        grid_spec=pltpu.PrefetchScalarGridSpec(
            num_scalar_prefetch=2,
            grid=(head_group,),
            in_specs=[full(seg_rows.shape), head, head] + [full((2, block_rows, head_dim))] * block_count,
            out_specs=[head] + [full((block_rows, 2 * head_dim))] * block_count,
            scratch_shapes=[
                pltpu.VMEM((2, key_count, head_dim), jnp.bfloat16),
                pltpu.VMEM((row_count, key_count), jnp.int32),
                pltpu.VMEM((key_count, head_dim), jnp.float32),
                pltpu.VMEM((key_count, head_dim), jnp.float32),
            ],
        ),
        out_shape=[jax.ShapeDtypeStruct((row_count, width), jnp.bfloat16)] + [part] * block_count,
        compiler_params=pltpu.CompilerParams(dimension_semantics=("arbitrary",)),
    )(block_order, rank, seg_rows, query_states, out_grad, *kv_blocks)
    return outs[0], outs[1:]


def body(
    block_order,
    segment_ids,
    layer_input,
    query_states,
    key_states,
    value_states,
    out_grad,
    master_weight,
    first_moment,
    second_moment,
):
    row_count, head_dim = key_states.shape
    head_group = query_states.shape[1] // head_dim
    ctx_count = lax.axis_size("ctx")
    roll_count = lax.axis_size("roll")
    ctx_rank = lax.axis_index("ctx")
    roll_rank = lax.axis_index("roll")
    score_scale = head_dim ** (-0.5)

    seg_table = segment_ids.reshape(ctx_count, row_count)

    own_kv = jnp.stack([key_states, value_states])
    kv_blocks = [own_kv] + [
        shifted(own_kv, "ctx", ctx_count, -s) for s in range(1, ctx_count)
    ]
    query_grad, part_blocks = attention_backward(
        block_order,
        jnp.reshape(ctx_rank, (1,)).astype(jnp.int32),
        seg_table,
        query_states,
        out_grad,
        kv_blocks,
        head_dim,
        score_scale,
    )

    kv_sum = part_blocks[0].astype(jnp.float32)
    for s in range(1, ctx_count):
        kv_sum = kv_sum + shifted(part_blocks[s], "ctx", ctx_count, s).astype(jnp.float32)
    key_value = kv_sum.astype(jnp.bfloat16)
    key_grad = key_value[:, :head_dim]

    owner_rows = master_weight.shape[0]
    picked = lax.dynamic_index_in_dim(
        layer_input.reshape(ctx_count, roll_count, owner_rows, row_count),
        roll_rank,
        1,
        keepdims=False,
    )
    products = jnp.einsum(
        "csr,rh->csh", picked, key_grad, preferred_element_type=jnp.float32
    ).astype(jnp.bfloat16)
    weight_grad = lax.dynamic_index_in_dim(products, ctx_rank, 0, keepdims=False).astype(
        jnp.float32
    )
    for s in range(1, ctx_count):
        outgoing = lax.dynamic_index_in_dim(
            products, (ctx_rank + s) % ctx_count, 0, keepdims=False
        )
        weight_grad = weight_grad + shifted(outgoing, "ctx", ctx_count, s).astype(jnp.float32)

    updated_first = BETA_ONE * first_moment + (1.0 - BETA_ONE) * weight_grad
    updated_second = BETA_TWO * second_moment + (1.0 - BETA_TWO) * weight_grad * weight_grad
    update = (
        updated_first / CORRECT_ONE / (jnp.sqrt(updated_second / CORRECT_TWO) + ADAM_EPS)
        + DECAY_RATE * master_weight
    )
    updated_master = master_weight - LEARN_RATE * update
    rollout_weight = lax.all_gather(updated_master.astype(jnp.bfloat16), "roll", axis=0, tiled=True)
    return (query_grad, key_value, updated_master, updated_first, updated_second, rollout_weight)


def solution(mesh):
    placed = (
        P(),
        P(),
        P(None, "ctx"),
        P("ctx", None),
        P("ctx", None),
        P("ctx", None),
        P("ctx", None),
        P(("ctx", "roll"), None),
        P(("ctx", "roll"), None),
        P(("ctx", "roll"), None),
    )
    return jax.shard_map(
        body,
        mesh=mesh,
        in_specs=placed,
        out_specs=(
            P("ctx", None),
            P("ctx", None),
            P(("ctx", "roll"), None),
            P(("ctx", "roll"), None),
            P(("ctx", "roll"), None),
            P("ctx", None),
        ),
        check_vma=False,
    )
```

```python
import functools

import jax
import jax.numpy as jnp
from jax import lax
from jax.experimental import pallas as pl
from jax.experimental.pallas import tpu as pltpu
from jax.sharding import PartitionSpec as P


NEG_FILL = -1e30
BETA_ONE = 0.9
BETA_TWO = 0.95
ADAM_EPS = 1e-08
DECAY_RATE = 0.1
LEARN_RATE = 1e-06
CORRECT_ONE = 0.9999734386011124
CORRECT_TWO = 0.994079470779666


def shifted(value, axis, count, shift):
    return lax.ppermute(value, axis, [(i, (i + shift) % count) for i in range(count)])


def attention_kernel(block_count, block_rows, head_dim, score_scale, *refs):
    order_ref, rank_ref, seg_ref, q_ref, do_ref = refs[:5]
    kv_refs = refs[5 : 5 + block_count]
    dq_ref = refs[5 + block_count]
    part_refs = refs[6 + block_count : 6 + 2 * block_count]
    key_scr, kt_scr, vt_scr, mask_scr, dk_acc, dv_acc = refs[6 + 2 * block_count :]
    step = pl.program_id(0)

    @pl.when(step == 0)
    def _():
        rank = rank_ref[0]
        lane = lax.broadcasted_iota(jnp.int32, (block_rows, block_rows), 1)
        sub = lax.broadcasted_iota(jnp.int32, (block_rows, block_rows), 0)
        own_seg = seg_ref[pl.ds(rank, 1), :]
        q_seg = jnp.sum(jnp.where(lane == sub, own_seg, 0), axis=1, keepdims=True)
        q_pos = order_ref[rank] * block_rows + sub[:, :1]
        for b in range(block_count):
            source = (rank + b) % block_count
            k_pos = order_ref[source] * block_rows + lane[:1, :]
            k_seg = seg_ref[pl.ds(source, 1), :]
            visible = (k_pos <= q_pos) & (k_seg == q_seg)
            cols = slice(b * block_rows, (b + 1) * block_rows)
            mask_scr[:, cols] = visible.astype(jnp.int32)
            key_block = kv_refs[b][0]
            key_scr[cols, :] = key_block
            kt_scr[:, cols] = key_block.astype(jnp.float32).T.astype(jnp.bfloat16)
            vt_scr[:, cols] = kv_refs[b][1].astype(jnp.float32).T.astype(jnp.bfloat16)
        dk_acc[...] = jnp.zeros_like(dk_acc)
        dv_acc[...] = jnp.zeros_like(dv_acc)

    q = q_ref[...]
    do = do_ref[...]
    visible = mask_scr[...] != 0
    scores = jnp.dot(q, kt_scr[...], preferred_element_type=jnp.float32) * score_scale
    scores = jnp.where(visible, scores, NEG_FILL)
    row_top = jnp.max(scores, axis=1, keepdims=True)
    expo = jnp.where(visible, jnp.exp(scores - row_top), 0.0)
    weights = expo * (1.0 / jnp.sum(expo, axis=1, keepdims=True))
    dprob = jnp.dot(do, vt_scr[...], preferred_element_type=jnp.float32)
    delta = jnp.sum(weights * dprob, axis=1, keepdims=True)
    dscore = weights * (dprob - delta)
    weights_half = weights.astype(jnp.bfloat16)
    dscore_half = dscore.astype(jnp.bfloat16)
    query_part = jnp.dot(dscore_half, key_scr[...], preferred_element_type=jnp.float32) * score_scale
    dq_ref[...] = query_part.astype(dq_ref.dtype)
    q_t = q.astype(jnp.float32).T.astype(jnp.bfloat16)
    do_t = do.astype(jnp.float32).T.astype(jnp.bfloat16)
    dk_acc[...] += jnp.dot(q_t, dscore_half, preferred_element_type=jnp.float32)
    dv_acc[...] += jnp.dot(do_t, weights_half, preferred_element_type=jnp.float32)

    @pl.when(step == pl.num_programs(0) - 1)
    def _():
        for b in range(block_count):
            cols = slice(b * block_rows, (b + 1) * block_rows)
            part_refs[b][:, :head_dim] = (dk_acc[:, cols].T * score_scale).astype(jnp.bfloat16)
            part_refs[b][:, head_dim:] = dv_acc[:, cols].T.astype(jnp.bfloat16)


def attention_backward(block_order, rank, seg_rows, query_states, out_grad, kv_blocks, head_dim, score_scale):
    row_count, width = query_states.shape
    head_group = width // head_dim
    block_count = len(kv_blocks)
    block_rows = kv_blocks[0].shape[1]
    key_count = block_count * block_rows
    full = lambda shape: pl.BlockSpec(shape, lambda h, *_: (0,) * len(shape))
    head = pl.BlockSpec((row_count, head_dim), lambda h, *_: (0, h))
    part = jax.ShapeDtypeStruct((block_rows, 2 * head_dim), jnp.bfloat16)
    kernel = functools.partial(attention_kernel, block_count, block_rows, head_dim, score_scale)
    outs = pl.pallas_call(
        kernel,
        grid_spec=pltpu.PrefetchScalarGridSpec(
            num_scalar_prefetch=2,
            grid=(head_group,),
            in_specs=[full(seg_rows.shape), head, head] + [full((2, block_rows, head_dim))] * block_count,
            out_specs=[head] + [full((block_rows, 2 * head_dim))] * block_count,
            scratch_shapes=[
                pltpu.VMEM((key_count, head_dim), jnp.bfloat16),
                pltpu.VMEM((head_dim, key_count), jnp.bfloat16),
                pltpu.VMEM((head_dim, key_count), jnp.bfloat16),
                pltpu.VMEM((row_count, key_count), jnp.int32),
                pltpu.VMEM((head_dim, key_count), jnp.float32),
                pltpu.VMEM((head_dim, key_count), jnp.float32),
            ],
        ),
        out_shape=[jax.ShapeDtypeStruct((row_count, width), jnp.bfloat16)] + [part] * block_count,
        compiler_params=pltpu.CompilerParams(dimension_semantics=("arbitrary",)),
    )(block_order, rank, seg_rows, query_states, out_grad, *kv_blocks)
    return outs[0], outs[1:]


def body(
    block_order,
    segment_ids,
    layer_input,
    query_states,
    key_states,
    value_states,
    out_grad,
    master_weight,
    first_moment,
    second_moment,
):
    row_count, head_dim = key_states.shape
    head_group = query_states.shape[1] // head_dim
    ctx_count = lax.axis_size("ctx")
    roll_count = lax.axis_size("roll")
    ctx_rank = lax.axis_index("ctx")
    roll_rank = lax.axis_index("roll")
    score_scale = head_dim ** (-0.5)

    seg_table = segment_ids.reshape(ctx_count, row_count)

    own_kv = jnp.stack([key_states, value_states])
    kv_blocks = [own_kv] + [
        shifted(own_kv, "ctx", ctx_count, -s) for s in range(1, ctx_count)
    ]
    query_grad, part_blocks = attention_backward(
        block_order,
        jnp.reshape(ctx_rank, (1,)).astype(jnp.int32),
        seg_table,
        query_states,
        out_grad,
        kv_blocks,
        head_dim,
        score_scale,
    )

    kv_sum = part_blocks[0].astype(jnp.float32)
    for s in range(1, ctx_count):
        kv_sum = kv_sum + shifted(part_blocks[s], "ctx", ctx_count, s).astype(jnp.float32)
    key_value = kv_sum.astype(jnp.bfloat16)
    key_grad = key_value[:, :head_dim]

    owner_rows = master_weight.shape[0]
    picked = lax.dynamic_index_in_dim(
        layer_input.reshape(ctx_count, roll_count, owner_rows, row_count),
        roll_rank,
        1,
        keepdims=False,
    )
    products = jnp.einsum(
        "csr,rh->csh", picked, key_grad, preferred_element_type=jnp.float32
    ).astype(jnp.bfloat16)
    weight_grad = lax.dynamic_index_in_dim(products, ctx_rank, 0, keepdims=False).astype(
        jnp.float32
    )
    for s in range(1, ctx_count):
        outgoing = lax.dynamic_index_in_dim(
            products, (ctx_rank + s) % ctx_count, 0, keepdims=False
        )
        weight_grad = weight_grad + shifted(outgoing, "ctx", ctx_count, s).astype(jnp.float32)

    updated_first = BETA_ONE * first_moment + (1.0 - BETA_ONE) * weight_grad
    updated_second = BETA_TWO * second_moment + (1.0 - BETA_TWO) * weight_grad * weight_grad
    update = (
        updated_first / CORRECT_ONE / (jnp.sqrt(updated_second / CORRECT_TWO) + ADAM_EPS)
        + DECAY_RATE * master_weight
    )
    updated_master = master_weight - LEARN_RATE * update
    rollout_weight = lax.all_gather(updated_master.astype(jnp.bfloat16), "roll", axis=0, tiled=True)
    return (query_grad, key_value, updated_master, updated_first, updated_second, rollout_weight)


def solution(mesh):
    placed = (
        P(),
        P(),
        P(None, "ctx"),
        P("ctx", None),
        P("ctx", None),
        P("ctx", None),
        P("ctx", None),
        P(("ctx", "roll"), None),
        P(("ctx", "roll"), None),
        P(("ctx", "roll"), None),
    )
    return jax.shard_map(
        body,
        mesh=mesh,
        in_specs=placed,
        out_specs=(
            P("ctx", None),
            P("ctx", None),
            P(("ctx", "roll"), None),
            P(("ctx", "roll"), None),
            P(("ctx", "roll"), None),
            P("ctx", None),
        ),
        check_vma=False,
    )
```

```python
import functools

import jax
import jax.numpy as jnp
from jax import lax
from jax.experimental import pallas as pl
from jax.experimental.pallas import tpu as pltpu
from jax.sharding import PartitionSpec as P


NEG_FILL = -1e30
BETA_ONE = 0.9
BETA_TWO = 0.95
ADAM_EPS = 1e-08
DECAY_RATE = 0.1
LEARN_RATE = 1e-06
CORRECT_ONE = 0.9999734386011124
CORRECT_TWO = 0.994079470779666


def shifted(value, axis, count, shift):
    return lax.ppermute(value, axis, [(i, (i + shift) % count) for i in range(count)])


def attention_kernel(block_count, block_rows, head_dim, score_scale, *refs):
    order_ref, rank_ref, seg_ref, q_ref, do_ref = refs[:5]
    kv_refs = refs[5 : 5 + block_count]
    dq_ref = refs[5 + block_count]
    part_refs = refs[6 + block_count : 6 + 2 * block_count]
    key_scr, kt_scr, vt_scr, mask_scr, dk_acc, dv_acc = refs[6 + 2 * block_count :]
    step = pl.program_id(0)

    @pl.when(step == 0)
    def _():
        rank = rank_ref[0]
        lane = lax.broadcasted_iota(jnp.int32, (block_rows, block_rows), 1)
        sub = lax.broadcasted_iota(jnp.int32, (block_rows, block_rows), 0)
        own_seg = seg_ref[pl.ds(rank, 1), :]
        q_seg = jnp.sum(jnp.where(lane == sub, own_seg, 0), axis=1, keepdims=True)
        q_pos = order_ref[rank] * block_rows + sub[:, :1]
        for b in range(block_count):
            source = (rank + b) % block_count
            k_pos = order_ref[source] * block_rows + lane[:1, :]
            k_seg = seg_ref[pl.ds(source, 1), :]
            visible = (k_pos <= q_pos) & (k_seg == q_seg)
            cols = slice(b * block_rows, (b + 1) * block_rows)
            mask_scr[:, cols] = visible.astype(jnp.int32)
            key_block = kv_refs[b][0]
            key_scr[cols, :] = key_block
            kt_scr[:, cols] = key_block.astype(jnp.float32).T.astype(jnp.bfloat16)
            vt_scr[:, cols] = kv_refs[b][1].astype(jnp.float32).T.astype(jnp.bfloat16)
        dk_acc[...] = jnp.zeros_like(dk_acc)
        dv_acc[...] = jnp.zeros_like(dv_acc)

    for h in range(q_ref.shape[1] // head_dim):
        heads = slice(h * head_dim, (h + 1) * head_dim)
        q = q_ref[:, heads]
        do = do_ref[:, heads]
        visible = mask_scr[...] != 0
        scores = jnp.dot(q, kt_scr[...], preferred_element_type=jnp.float32) * score_scale
        scores = jnp.where(visible, scores, NEG_FILL)
        row_top = jnp.max(scores, axis=1, keepdims=True)
        expo = jnp.where(visible, jnp.exp(scores - row_top), 0.0)
        weights = expo * (1.0 / jnp.sum(expo, axis=1, keepdims=True))
        dprob = jnp.dot(do, vt_scr[...], preferred_element_type=jnp.float32)
        delta = jnp.sum(weights * dprob, axis=1, keepdims=True)
        dscore = weights * (dprob - delta)
        weights_half = weights.astype(jnp.bfloat16)
        dscore_half = dscore.astype(jnp.bfloat16)
        query_part = jnp.dot(dscore_half, key_scr[...], preferred_element_type=jnp.float32) * score_scale
        dq_ref[:, heads] = query_part.astype(dq_ref.dtype)
        q_t = q.astype(jnp.float32).T.astype(jnp.bfloat16)
        do_t = do.astype(jnp.float32).T.astype(jnp.bfloat16)
        dk_acc[...] += jnp.dot(q_t, dscore_half, preferred_element_type=jnp.float32)
        dv_acc[...] += jnp.dot(do_t, weights_half, preferred_element_type=jnp.float32)

    @pl.when(step == pl.num_programs(0) - 1)
    def _():
        for b in range(block_count):
            cols = slice(b * block_rows, (b + 1) * block_rows)
            part_refs[b][:, :head_dim] = (dk_acc[:, cols].T * score_scale).astype(jnp.bfloat16)
            part_refs[b][:, head_dim:] = dv_acc[:, cols].T.astype(jnp.bfloat16)


def attention_backward(block_order, rank, seg_rows, query_states, out_grad, kv_blocks, head_dim, score_scale):
    row_count, width = query_states.shape
    head_group = width // head_dim
    block_count = len(kv_blocks)
    block_rows = kv_blocks[0].shape[1]
    key_count = block_count * block_rows
    full = lambda shape: pl.BlockSpec(shape, lambda h, *_: (0,) * len(shape))
    head = pl.BlockSpec((row_count, width), lambda h, *_: (0, 0))
    part = jax.ShapeDtypeStruct((block_rows, 2 * head_dim), jnp.bfloat16)
    kernel = functools.partial(attention_kernel, block_count, block_rows, head_dim, score_scale)
    outs = pl.pallas_call(
        kernel,
        grid_spec=pltpu.PrefetchScalarGridSpec(
            num_scalar_prefetch=2,
            grid=(1,),
            in_specs=[full(seg_rows.shape), head, head] + [full((2, block_rows, head_dim))] * block_count,
            out_specs=[head] + [full((block_rows, 2 * head_dim))] * block_count,
            scratch_shapes=[
                pltpu.VMEM((key_count, head_dim), jnp.bfloat16),
                pltpu.VMEM((head_dim, key_count), jnp.bfloat16),
                pltpu.VMEM((head_dim, key_count), jnp.bfloat16),
                pltpu.VMEM((row_count, key_count), jnp.int32),
                pltpu.VMEM((head_dim, key_count), jnp.float32),
                pltpu.VMEM((head_dim, key_count), jnp.float32),
            ],
        ),
        out_shape=[jax.ShapeDtypeStruct((row_count, width), jnp.bfloat16)] + [part] * block_count,
        compiler_params=pltpu.CompilerParams(dimension_semantics=("arbitrary",)),
    )(block_order, rank, seg_rows, query_states, out_grad, *kv_blocks)
    return outs[0], outs[1:]


def body(
    block_order,
    segment_ids,
    layer_input,
    query_states,
    key_states,
    value_states,
    out_grad,
    master_weight,
    first_moment,
    second_moment,
):
    row_count, head_dim = key_states.shape
    head_group = query_states.shape[1] // head_dim
    ctx_count = lax.axis_size("ctx")
    roll_count = lax.axis_size("roll")
    ctx_rank = lax.axis_index("ctx")
    roll_rank = lax.axis_index("roll")
    score_scale = head_dim ** (-0.5)

    seg_table = segment_ids.reshape(ctx_count, row_count)

    own_kv = jnp.stack([key_states, value_states])
    kv_blocks = [own_kv] + [
        shifted(own_kv, "ctx", ctx_count, -s) for s in range(1, ctx_count)
    ]
    query_grad, part_blocks = attention_backward(
        block_order,
        jnp.reshape(ctx_rank, (1,)).astype(jnp.int32),
        seg_table,
        query_states,
        out_grad,
        kv_blocks,
        head_dim,
        score_scale,
    )

    kv_sum = part_blocks[0].astype(jnp.float32)
    for s in range(1, ctx_count):
        kv_sum = kv_sum + shifted(part_blocks[s], "ctx", ctx_count, s).astype(jnp.float32)
    key_value = kv_sum.astype(jnp.bfloat16)
    key_grad = key_value[:, :head_dim]

    owner_rows = master_weight.shape[0]
    picked = lax.dynamic_index_in_dim(
        layer_input.reshape(ctx_count, roll_count, owner_rows, row_count),
        roll_rank,
        1,
        keepdims=False,
    )
    products = jnp.einsum(
        "csr,rh->csh", picked, key_grad, preferred_element_type=jnp.float32
    ).astype(jnp.bfloat16)
    weight_grad = lax.dynamic_index_in_dim(products, ctx_rank, 0, keepdims=False).astype(
        jnp.float32
    )
    for s in range(1, ctx_count):
        outgoing = lax.dynamic_index_in_dim(
            products, (ctx_rank + s) % ctx_count, 0, keepdims=False
        )
        weight_grad = weight_grad + shifted(outgoing, "ctx", ctx_count, s).astype(jnp.float32)

    updated_first = BETA_ONE * first_moment + (1.0 - BETA_ONE) * weight_grad
    updated_second = BETA_TWO * second_moment + (1.0 - BETA_TWO) * weight_grad * weight_grad
    update = (
        updated_first / CORRECT_ONE / (jnp.sqrt(updated_second / CORRECT_TWO) + ADAM_EPS)
        + DECAY_RATE * master_weight
    )
    updated_master = master_weight - LEARN_RATE * update
    rollout_weight = lax.all_gather(updated_master.astype(jnp.bfloat16), "roll", axis=0, tiled=True)
    return (query_grad, key_value, updated_master, updated_first, updated_second, rollout_weight)


def solution(mesh):
    placed = (
        P(),
        P(),
        P(None, "ctx"),
        P("ctx", None),
        P("ctx", None),
        P("ctx", None),
        P("ctx", None),
        P(("ctx", "roll"), None),
        P(("ctx", "roll"), None),
        P(("ctx", "roll"), None),
    )
    return jax.shard_map(
        body,
        mesh=mesh,
        in_specs=placed,
        out_specs=(
            P("ctx", None),
            P("ctx", None),
            P(("ctx", "roll"), None),
            P(("ctx", "roll"), None),
            P(("ctx", "roll"), None),
            P("ctx", None),
        ),
        check_vma=False,
    )
```

```python
import functools

import jax
import jax.numpy as jnp
from jax import lax
from jax.experimental import pallas as pl
from jax.experimental.pallas import tpu as pltpu
from jax.sharding import PartitionSpec as P


NEG_FILL = -1e30
BETA_ONE = 0.9
BETA_TWO = 0.95
ADAM_EPS = 1e-08
DECAY_RATE = 0.1
LEARN_RATE = 1e-06
CORRECT_ONE = 0.9999734386011124
CORRECT_TWO = 0.994079470779666


def shifted(value, axis, count, shift):
    return lax.ppermute(value, axis, [(i, (i + shift) % count) for i in range(count)])


def attention_kernel(block_count, block_rows, head_dim, score_scale, *refs):
    order_ref, rank_ref, seg_ref, q_ref, do_ref = refs[:5]
    kv_refs = refs[5 : 5 + block_count]
    dq_ref = refs[5 + block_count]
    part_refs = refs[6 + block_count : 6 + 2 * block_count]
    key_scr, kt_scr, vt_scr, mask_scr, dk_acc, dv_acc = refs[6 + 2 * block_count :]
    step = pl.program_id(0)

    @pl.when(step == 0)
    def _():
        rank = rank_ref[0]
        lane = lax.broadcasted_iota(jnp.int32, (block_rows, block_rows), 1)
        sub = lax.broadcasted_iota(jnp.int32, (block_rows, block_rows), 0)
        own_seg = seg_ref[pl.ds(rank, 1), :]
        q_seg = jnp.sum(jnp.where(lane == sub, own_seg, 0), axis=1, keepdims=True)
        q_pos = order_ref[rank] * block_rows + sub[:, :1]
        for b in range(block_count):
            source = (rank + b) % block_count
            k_pos = order_ref[source] * block_rows + lane[:1, :]
            k_seg = seg_ref[pl.ds(source, 1), :]
            visible = (k_pos <= q_pos) & (k_seg == q_seg)
            cols = slice(b * block_rows, (b + 1) * block_rows)
            mask_scr[:, cols] = visible.astype(jnp.int32)
            key_block = kv_refs[b][0]
            key_scr[cols, :] = key_block
            kt_scr[:, cols] = key_block.astype(jnp.float32).T.astype(jnp.bfloat16)
            vt_scr[:, cols] = kv_refs[b][1].astype(jnp.float32).T.astype(jnp.bfloat16)
        dk_acc[...] = jnp.zeros_like(dk_acc)
        dv_acc[...] = jnp.zeros_like(dv_acc)

    for h in range(q_ref.shape[1] // head_dim):
        heads = slice(h * head_dim, (h + 1) * head_dim)
        q = q_ref[:, heads]
        do = do_ref[:, heads]
        visible = mask_scr[...] != 0
        scores = jnp.dot(q, kt_scr[...], preferred_element_type=jnp.float32) * score_scale
        scores = jnp.where(visible, scores, NEG_FILL)
        row_top = jnp.max(scores, axis=1, keepdims=True)
        expo = jnp.where(visible, jnp.exp(scores - row_top), 0.0)
        weights = expo * (1.0 / jnp.sum(expo, axis=1, keepdims=True))
        dprob = jnp.dot(do, vt_scr[...], preferred_element_type=jnp.float32)
        delta = jnp.sum(weights * dprob, axis=1, keepdims=True)
        dscore = weights * (dprob - delta)
        weights_half = weights.astype(jnp.bfloat16)
        dscore_half = dscore.astype(jnp.bfloat16)
        query_part = jnp.dot(dscore_half, key_scr[...], preferred_element_type=jnp.float32) * score_scale
        dq_ref[:, heads] = query_part.astype(dq_ref.dtype)
        q_t = q.astype(jnp.float32).T.astype(jnp.bfloat16)
        do_t = do.astype(jnp.float32).T.astype(jnp.bfloat16)
        dk_acc[...] += jnp.dot(q_t, dscore_half, preferred_element_type=jnp.float32)
        dv_acc[...] += jnp.dot(do_t, weights_half, preferred_element_type=jnp.float32)

    @pl.when(step == pl.num_programs(0) - 1)
    def _():
        for b in range(block_count):
            cols = slice(b * block_rows, (b + 1) * block_rows)
            part_refs[b][:, :head_dim] = (dk_acc[:, cols].T * score_scale).astype(jnp.bfloat16)
            part_refs[b][:, head_dim:] = dv_acc[:, cols].T.astype(jnp.bfloat16)


def attention_backward(block_order, rank, seg_rows, query_states, out_grad, kv_blocks, head_dim, score_scale):
    row_count, width = query_states.shape
    head_group = width // head_dim
    block_count = len(kv_blocks)
    block_rows = kv_blocks[0].shape[1]
    key_count = block_count * block_rows
    full = lambda shape: pl.BlockSpec(shape, lambda h, *_: (0,) * len(shape))
    head = pl.BlockSpec((row_count, width), lambda h, *_: (0, 0))
    part = jax.ShapeDtypeStruct((block_rows, 2 * head_dim), jnp.bfloat16)
    kernel = functools.partial(attention_kernel, block_count, block_rows, head_dim, score_scale)
    outs = pl.pallas_call(
        kernel,
        grid_spec=pltpu.PrefetchScalarGridSpec(
            num_scalar_prefetch=2,
            grid=(1,),
            in_specs=[full(seg_rows.shape), head, head] + [full((2, block_rows, head_dim))] * block_count,
            out_specs=[head] + [full((block_rows, 2 * head_dim))] * block_count,
            scratch_shapes=[
                pltpu.VMEM((key_count, head_dim), jnp.bfloat16),
                pltpu.VMEM((head_dim, key_count), jnp.bfloat16),
                pltpu.VMEM((head_dim, key_count), jnp.bfloat16),
                pltpu.VMEM((row_count, key_count), jnp.int32),
                pltpu.VMEM((head_dim, key_count), jnp.float32),
                pltpu.VMEM((head_dim, key_count), jnp.float32),
            ],
        ),
        out_shape=[jax.ShapeDtypeStruct((row_count, width), jnp.bfloat16)] + [part] * block_count,
        compiler_params=pltpu.CompilerParams(dimension_semantics=("arbitrary",)),
    )(block_order, rank, seg_rows, query_states, out_grad, *kv_blocks)
    return outs[0], outs[1:]


def middle_kernel(block_count, head_dim, *refs):
    rank_ref, roll_ref, rows_ref = refs[:3]
    part_refs = refs[3 : 3 + block_count]
    kv_ref = refs[3 + block_count]
    out_refs = refs[4 + block_count :]
    total = part_refs[0][...].astype(jnp.float32)
    for b in range(1, block_count):
        total = total + part_refs[b][...].astype(jnp.float32)
    key_value = total.astype(jnp.bfloat16)
    kv_ref[...] = key_value
    key_grad = key_value[:, :head_dim]
    rank = rank_ref[0]
    for s in range(block_count):
        rows = rows_ref[(rank + s) % block_count]
        out_refs[s][...] = jnp.dot(rows, key_grad, preferred_element_type=jnp.float32).astype(jnp.bfloat16)


def key_value_and_products(rank, roll_rank, layer_input, part_blocks, roll_count, owner_rows):
    block_count = len(part_blocks)
    row_count, width = part_blocks[0].shape
    head_dim = width // 2
    features = layer_input.reshape(block_count, roll_count, owner_rows, row_count)
    full = lambda shape: pl.BlockSpec(shape, lambda i, *_: (0,) * len(shape))
    picked = pl.BlockSpec((block_count, None, owner_rows, row_count), lambda i, rank_ref, roll_ref: (0, roll_ref[0], 0, 0))
    product = jax.ShapeDtypeStruct((owner_rows, head_dim), jnp.bfloat16)
    outs = pl.pallas_call(
        functools.partial(middle_kernel, block_count, head_dim),
        grid_spec=pltpu.PrefetchScalarGridSpec(
            num_scalar_prefetch=2,
            grid=(1,),
            in_specs=[picked] + [full((row_count, width))] * block_count,
            out_specs=[full((row_count, width))] + [full((owner_rows, head_dim))] * block_count,
        ),
        out_shape=[jax.ShapeDtypeStruct((row_count, width), jnp.bfloat16)] + [product] * block_count,
    )(rank, roll_rank, features, *part_blocks)
    return outs[0], outs[1:]


def body(
    block_order,
    segment_ids,
    layer_input,
    query_states,
    key_states,
    value_states,
    out_grad,
    master_weight,
    first_moment,
    second_moment,
):
    row_count, head_dim = key_states.shape
    head_group = query_states.shape[1] // head_dim
    ctx_count = lax.axis_size("ctx")
    roll_count = lax.axis_size("roll")
    ctx_rank = lax.axis_index("ctx")
    roll_rank = lax.axis_index("roll")
    score_scale = head_dim ** (-0.5)

    seg_table = segment_ids.reshape(ctx_count, row_count)
    rank_vector = jnp.reshape(ctx_rank, (1,)).astype(jnp.int32)

    own_kv = jnp.stack([key_states, value_states])
    kv_blocks = [own_kv] + [
        shifted(own_kv, "ctx", ctx_count, -s) for s in range(1, ctx_count)
    ]
    query_grad, part_blocks = attention_backward(
        block_order,
        rank_vector,
        seg_table,
        query_states,
        out_grad,
        kv_blocks,
        head_dim,
        score_scale,
    )

    received = [part_blocks[0]] + [
        shifted(part_blocks[s], "ctx", ctx_count, s) for s in range(1, ctx_count)
    ]
    owner_rows = master_weight.shape[0]
    key_value, products = key_value_and_products(
        rank_vector,
        jnp.reshape(roll_rank, (1,)).astype(jnp.int32),
        layer_input,
        received,
        roll_count,
        owner_rows,
    )
    weight_grad = products[0].astype(jnp.float32)
    for s in range(1, ctx_count):
        weight_grad = weight_grad + shifted(products[s], "ctx", ctx_count, s).astype(jnp.float32)

    updated_first = BETA_ONE * first_moment + (1.0 - BETA_ONE) * weight_grad
    updated_second = BETA_TWO * second_moment + (1.0 - BETA_TWO) * weight_grad * weight_grad
    update = (
        updated_first / CORRECT_ONE / (jnp.sqrt(updated_second / CORRECT_TWO) + ADAM_EPS)
        + DECAY_RATE * master_weight
    )
    updated_master = master_weight - LEARN_RATE * update
    rollout_weight = lax.all_gather(updated_master.astype(jnp.bfloat16), "roll", axis=0, tiled=True)
    return (query_grad, key_value, updated_master, updated_first, updated_second, rollout_weight)


def solution(mesh):
    placed = (
        P(),
        P(),
        P(None, "ctx"),
        P("ctx", None),
        P("ctx", None),
        P("ctx", None),
        P("ctx", None),
        P(("ctx", "roll"), None),
        P(("ctx", "roll"), None),
        P(("ctx", "roll"), None),
    )
    return jax.shard_map(
        body,
        mesh=mesh,
        in_specs=placed,
        out_specs=(
            P("ctx", None),
            P("ctx", None),
            P(("ctx", "roll"), None),
            P(("ctx", "roll"), None),
            P(("ctx", "roll"), None),
            P("ctx", None),
        ),
        check_vma=False,
    )
```

```python
import functools

import jax
import jax.numpy as jnp
from jax import lax
from jax.experimental import pallas as pl
from jax.experimental.pallas import tpu as pltpu
from jax.sharding import PartitionSpec as P


NEG_FILL = -1e30
BETA_ONE = 0.9
BETA_TWO = 0.95
ADAM_EPS = 1e-08
DECAY_RATE = 0.1
LEARN_RATE = 1e-06
CORRECT_ONE = 0.9999734386011124
CORRECT_TWO = 0.994079470779666


def shifted(value, axis, count, shift):
    return lax.ppermute(value, axis, [(i, (i + shift) % count) for i in range(count)])


def attention_kernel(block_count, block_rows, head_dim, score_scale, *refs):
    order_ref, rank_ref, seg_ref, q_ref, do_ref, own_ref, gathered_ref = refs[:7]
    replicas = gathered_ref.shape[0]
    dq_ref = refs[7]
    part_refs = refs[8 : 8 + block_count]
    key_scr, kt_scr, vt_scr, mask_scr, dk_acc, dv_acc = refs[8 + block_count :]

    def kv_block(b, which):
        if b == 0:
            return own_ref[which]
        return gathered_ref[(b - 1) % replicas, (b - 1) // replicas, which]

    step = pl.program_id(0)

    @pl.when(step == 0)
    def _():
        rank = rank_ref[0]
        lane = lax.broadcasted_iota(jnp.int32, (block_rows, block_rows), 1)
        sub = lax.broadcasted_iota(jnp.int32, (block_rows, block_rows), 0)
        own_seg = seg_ref[pl.ds(rank, 1), :]
        q_seg = jnp.sum(jnp.where(lane == sub, own_seg, 0), axis=1, keepdims=True)
        q_pos = order_ref[rank] * block_rows + sub[:, :1]
        for b in range(block_count):
            source = (rank + b) % block_count
            k_pos = order_ref[source] * block_rows + lane[:1, :]
            k_seg = seg_ref[pl.ds(source, 1), :]
            visible = (k_pos <= q_pos) & (k_seg == q_seg)
            cols = slice(b * block_rows, (b + 1) * block_rows)
            mask_scr[:, cols] = visible.astype(jnp.int32)
            key_block = kv_block(b, 0)
            key_scr[cols, :] = key_block
            kt_scr[:, cols] = key_block.astype(jnp.float32).T.astype(jnp.bfloat16)
            vt_scr[:, cols] = kv_block(b, 1).astype(jnp.float32).T.astype(jnp.bfloat16)
        dk_acc[...] = jnp.zeros_like(dk_acc)
        dv_acc[...] = jnp.zeros_like(dv_acc)

    for h in range(q_ref.shape[1] // head_dim):
        heads = slice(h * head_dim, (h + 1) * head_dim)
        q = q_ref[:, heads]
        do = do_ref[:, heads]
        visible = mask_scr[...] != 0
        scores = jnp.dot(q, kt_scr[...], preferred_element_type=jnp.float32) * score_scale
        scores = jnp.where(visible, scores, NEG_FILL)
        row_top = jnp.max(scores, axis=1, keepdims=True)
        expo = jnp.where(visible, jnp.exp(scores - row_top), 0.0)
        weights = expo * (1.0 / jnp.sum(expo, axis=1, keepdims=True))
        dprob = jnp.dot(do, vt_scr[...], preferred_element_type=jnp.float32)
        delta = jnp.sum(weights * dprob, axis=1, keepdims=True)
        dscore = weights * (dprob - delta)
        weights_half = weights.astype(jnp.bfloat16)
        dscore_half = dscore.astype(jnp.bfloat16)
        query_part = jnp.dot(dscore_half, key_scr[...], preferred_element_type=jnp.float32) * score_scale
        dq_ref[:, heads] = query_part.astype(dq_ref.dtype)
        q_t = q.astype(jnp.float32).T.astype(jnp.bfloat16)
        do_t = do.astype(jnp.float32).T.astype(jnp.bfloat16)
        dk_acc[...] += jnp.dot(q_t, dscore_half, preferred_element_type=jnp.float32)
        dv_acc[...] += jnp.dot(do_t, weights_half, preferred_element_type=jnp.float32)

    @pl.when(step == pl.num_programs(0) - 1)
    def _():
        for b in range(block_count):
            cols = slice(b * block_rows, (b + 1) * block_rows)
            part_refs[b][:, :head_dim] = (dk_acc[:, cols].T * score_scale).astype(jnp.bfloat16)
            part_refs[b][:, head_dim:] = dv_acc[:, cols].T.astype(jnp.bfloat16)


def attention_backward(block_order, rank, seg_rows, query_states, out_grad, own_kv, gathered, head_dim, score_scale):
    row_count, width = query_states.shape
    head_group = width // head_dim
    block_count = seg_rows.shape[0]
    block_rows = own_kv.shape[1]
    key_count = block_count * block_rows
    full = lambda shape: pl.BlockSpec(shape, lambda h, *_: (0,) * len(shape))
    head = pl.BlockSpec((row_count, width), lambda h, *_: (0, 0))
    part = jax.ShapeDtypeStruct((block_rows, 2 * head_dim), jnp.bfloat16)
    kernel = functools.partial(attention_kernel, block_count, block_rows, head_dim, score_scale)
    outs = pl.pallas_call(
        kernel,
        grid_spec=pltpu.PrefetchScalarGridSpec(
            num_scalar_prefetch=2,
            grid=(1,),
            in_specs=[full(seg_rows.shape), head, head, full(own_kv.shape), full(gathered.shape)],
            out_specs=[head] + [full((block_rows, 2 * head_dim))] * block_count,
            scratch_shapes=[
                pltpu.VMEM((key_count, head_dim), jnp.bfloat16),
                pltpu.VMEM((head_dim, key_count), jnp.bfloat16),
                pltpu.VMEM((head_dim, key_count), jnp.bfloat16),
                pltpu.VMEM((row_count, key_count), jnp.int32),
                pltpu.VMEM((head_dim, key_count), jnp.float32),
                pltpu.VMEM((head_dim, key_count), jnp.float32),
            ],
        ),
        out_shape=[jax.ShapeDtypeStruct((row_count, width), jnp.bfloat16)] + [part] * block_count,
        compiler_params=pltpu.CompilerParams(dimension_semantics=("arbitrary",)),
    )(block_order, rank, seg_rows, query_states, out_grad, own_kv, gathered)
    return outs[0], outs[1:]


def middle_kernel(block_count, head_dim, *refs):
    rank_ref, roll_ref, rows_ref = refs[:3]
    part_refs = refs[3 : 3 + block_count]
    kv_ref = refs[3 + block_count]
    out_refs = refs[4 + block_count :]
    total = part_refs[0][...].astype(jnp.float32)
    for b in range(1, block_count):
        total = total + part_refs[b][...].astype(jnp.float32)
    key_value = total.astype(jnp.bfloat16)
    kv_ref[...] = key_value
    key_grad = key_value[:, :head_dim]
    rank = rank_ref[0]
    for s in range(block_count):
        rows = rows_ref[(rank + s) % block_count]
        out_refs[s][...] = jnp.dot(rows, key_grad, preferred_element_type=jnp.float32).astype(jnp.bfloat16)


def key_value_and_products(rank, roll_rank, layer_input, part_blocks, roll_count, owner_rows):
    block_count = len(part_blocks)
    row_count, width = part_blocks[0].shape
    head_dim = width // 2
    features = layer_input.reshape(block_count, roll_count, owner_rows, row_count)
    full = lambda shape: pl.BlockSpec(shape, lambda i, *_: (0,) * len(shape))
    picked = pl.BlockSpec((block_count, None, owner_rows, row_count), lambda i, rank_ref, roll_ref: (0, roll_ref[0], 0, 0))
    product = jax.ShapeDtypeStruct((owner_rows, head_dim), jnp.bfloat16)
    outs = pl.pallas_call(
        functools.partial(middle_kernel, block_count, head_dim),
        grid_spec=pltpu.PrefetchScalarGridSpec(
            num_scalar_prefetch=2,
            grid=(1,),
            in_specs=[picked] + [full((row_count, width))] * block_count,
            out_specs=[full((row_count, width))] + [full((owner_rows, head_dim))] * block_count,
        ),
        out_shape=[jax.ShapeDtypeStruct((row_count, width), jnp.bfloat16)] + [product] * block_count,
    )(rank, roll_rank, features, *part_blocks)
    return outs[0], outs[1:]


def body(
    block_order,
    segment_ids,
    layer_input,
    query_states,
    key_states,
    value_states,
    out_grad,
    master_weight,
    first_moment,
    second_moment,
):
    row_count, head_dim = key_states.shape
    head_group = query_states.shape[1] // head_dim
    ctx_count = lax.axis_size("ctx")
    roll_count = lax.axis_size("roll")
    ctx_rank = lax.axis_index("ctx")
    roll_rank = lax.axis_index("roll")
    score_scale = head_dim ** (-0.5)

    seg_table = segment_ids.reshape(ctx_count, row_count)
    rank_vector = jnp.reshape(ctx_rank, (1,)).astype(jnp.int32)

    own_kv = jnp.stack([key_states, value_states])
    rounds = -(-(ctx_count - 1) // roll_count)
    fetched = []
    for k in range(rounds):
        pairs = []
        for c in range(ctx_count):
            for r in range(roll_count):
                s = 1 + r + k * roll_count
                if s < ctx_count:
                    pairs.append((c * roll_count + r, ((c - s) % ctx_count) * roll_count + r))
        fetched.append(lax.ppermute(own_kv, ("ctx", "roll"), pairs))
    gathered = lax.all_gather(jnp.stack(fetched), "roll", axis=0, tiled=False)
    query_grad, part_blocks = attention_backward(
        block_order,
        rank_vector,
        seg_table,
        query_states,
        out_grad,
        own_kv,
        gathered,
        head_dim,
        score_scale,
    )

    received = [part_blocks[0]] + [
        shifted(part_blocks[s], "ctx", ctx_count, s) for s in range(1, ctx_count)
    ]
    owner_rows = master_weight.shape[0]
    key_value, products = key_value_and_products(
        rank_vector,
        jnp.reshape(roll_rank, (1,)).astype(jnp.int32),
        layer_input,
        received,
        roll_count,
        owner_rows,
    )
    weight_grad = products[0].astype(jnp.float32)
    for s in range(1, ctx_count):
        weight_grad = weight_grad + shifted(products[s], "ctx", ctx_count, s).astype(jnp.float32)

    updated_first = BETA_ONE * first_moment + (1.0 - BETA_ONE) * weight_grad
    updated_second = BETA_TWO * second_moment + (1.0 - BETA_TWO) * weight_grad * weight_grad
    update = (
        updated_first / CORRECT_ONE / (jnp.sqrt(updated_second / CORRECT_TWO) + ADAM_EPS)
        + DECAY_RATE * master_weight
    )
    updated_master = master_weight - LEARN_RATE * update
    rollout_weight = lax.all_gather(updated_master.astype(jnp.bfloat16), "roll", axis=0, tiled=True)
    return (query_grad, key_value, updated_master, updated_first, updated_second, rollout_weight)


def solution(mesh):
    placed = (
        P(),
        P(),
        P(None, "ctx"),
        P("ctx", None),
        P("ctx", None),
        P("ctx", None),
        P("ctx", None),
        P(("ctx", "roll"), None),
        P(("ctx", "roll"), None),
        P(("ctx", "roll"), None),
    )
    return jax.shard_map(
        body,
        mesh=mesh,
        in_specs=placed,
        out_specs=(
            P("ctx", None),
            P("ctx", None),
            P(("ctx", "roll"), None),
            P(("ctx", "roll"), None),
            P(("ctx", "roll"), None),
            P("ctx", None),
        ),
        check_vma=False,
    )
```

```python
import functools

import jax
import jax.numpy as jnp
from jax import lax
from jax.experimental import pallas as pl
from jax.experimental.pallas import tpu as pltpu
from jax.sharding import PartitionSpec as P


NEG_FILL = -1e30
BETA_ONE = 0.9
BETA_TWO = 0.95
ADAM_EPS = 1e-08
DECAY_RATE = 0.1
LEARN_RATE = 1e-06
CORRECT_ONE = 0.9999734386011124
CORRECT_TWO = 0.994079470779666


def shifted(value, axis, count, shift):
    return lax.ppermute(value, axis, [(i, (i + shift) % count) for i in range(count)])


def attention_kernel(block_count, block_rows, head_dim, score_scale, *refs):
    order_ref, rank_ref, seg_ref, q_ref, do_ref = refs[:5]
    kv_refs = refs[5 : 5 + block_count]
    dq_ref = refs[5 + block_count]
    part_refs = refs[6 + block_count : 6 + 2 * block_count]
    key_scr, kt_scr, vt_scr, mask_scr, dk_acc, dv_acc = refs[6 + 2 * block_count :]
    step = pl.program_id(0)

    @pl.when(step == 0)
    def _():
        rank = rank_ref[0]
        lane = lax.broadcasted_iota(jnp.int32, (block_rows, block_rows), 1)
        sub = lax.broadcasted_iota(jnp.int32, (block_rows, block_rows), 0)
        own_seg = seg_ref[pl.ds(rank, 1), :]
        q_seg = jnp.sum(jnp.where(lane == sub, own_seg, 0), axis=1, keepdims=True)
        q_pos = order_ref[rank] * block_rows + sub[:, :1]
        for b in range(block_count):
            source = (rank + b) % block_count
            k_pos = order_ref[source] * block_rows + lane[:1, :]
            k_seg = seg_ref[pl.ds(source, 1), :]
            visible = (k_pos <= q_pos) & (k_seg == q_seg)
            cols = slice(b * block_rows, (b + 1) * block_rows)
            mask_scr[:, cols] = visible.astype(jnp.int32)
            key_block = kv_refs[b][0]
            key_scr[cols, :] = key_block
            kt_scr[:, cols] = key_block.astype(jnp.float32).T.astype(jnp.bfloat16)
            vt_scr[:, cols] = kv_refs[b][1].astype(jnp.float32).T.astype(jnp.bfloat16)
        dk_acc[...] = jnp.zeros_like(dk_acc)
        dv_acc[...] = jnp.zeros_like(dv_acc)

    head_count = q_ref.shape[1] // head_dim
    key_count = block_count * block_rows
    pair = max(
        g for g in range(1, head_count + 1)
        if head_count % g == 0 and g * q_ref.shape[0] * key_count <= 768 * 1024
    ) if q_ref.shape[0] * key_count <= 768 * 1024 else 1
    visible_rows = mask_scr[...] != 0
    visible = jnp.concatenate([visible_rows] * pair, axis=0) if pair > 1 else visible_rows
    for h in range(0, head_count, pair):
        head_cols = [slice((h + i) * head_dim, (h + i + 1) * head_dim) for i in range(pair)]
        q = jnp.concatenate([q_ref[:, c] for c in head_cols], axis=0) if pair > 1 else q_ref[:, head_cols[0]]
        do = jnp.concatenate([do_ref[:, c] for c in head_cols], axis=0) if pair > 1 else do_ref[:, head_cols[0]]
        scores = jnp.dot(q, kt_scr[...], preferred_element_type=jnp.float32) * score_scale
        scores = jnp.where(visible, scores, NEG_FILL)
        row_top = jnp.max(scores, axis=1, keepdims=True)
        expo = jnp.where(visible, jnp.exp(scores - row_top), 0.0)
        weights = expo * (1.0 / jnp.sum(expo, axis=1, keepdims=True))
        dprob = jnp.dot(do, vt_scr[...], preferred_element_type=jnp.float32)
        delta = jnp.sum(weights * dprob, axis=1, keepdims=True)
        dscore = weights * (dprob - delta)
        weights_half = weights.astype(jnp.bfloat16)
        dscore_half = dscore.astype(jnp.bfloat16)
        query_part = jnp.dot(dscore_half, key_scr[...], preferred_element_type=jnp.float32) * score_scale
        rows = query_part.shape[0] // pair
        for i, c in enumerate(head_cols):
            dq_ref[:, c] = query_part[i * rows : (i + 1) * rows].astype(dq_ref.dtype)
        q_t = q.astype(jnp.float32).T.astype(jnp.bfloat16)
        do_t = do.astype(jnp.float32).T.astype(jnp.bfloat16)
        dk_acc[...] += jnp.dot(q_t, dscore_half, preferred_element_type=jnp.float32)
        dv_acc[...] += jnp.dot(do_t, weights_half, preferred_element_type=jnp.float32)

    @pl.when(step == pl.num_programs(0) - 1)
    def _():
        for b in range(block_count):
            cols = slice(b * block_rows, (b + 1) * block_rows)
            part_refs[b][:, :head_dim] = (dk_acc[:, cols].T * score_scale).astype(jnp.bfloat16)
            part_refs[b][:, head_dim:] = dv_acc[:, cols].T.astype(jnp.bfloat16)


def attention_backward(block_order, rank, seg_rows, query_states, out_grad, kv_blocks, head_dim, score_scale):
    row_count, width = query_states.shape
    head_group = width // head_dim
    block_count = len(kv_blocks)
    block_rows = kv_blocks[0].shape[1]
    key_count = block_count * block_rows
    full = lambda shape: pl.BlockSpec(shape, lambda h, *_: (0,) * len(shape))
    head = pl.BlockSpec((row_count, width), lambda h, *_: (0, 0))
    part = jax.ShapeDtypeStruct((block_rows, 2 * head_dim), jnp.bfloat16)
    kernel = functools.partial(attention_kernel, block_count, block_rows, head_dim, score_scale)
    outs = pl.pallas_call(
        kernel,
        grid_spec=pltpu.PrefetchScalarGridSpec(
            num_scalar_prefetch=2,
            grid=(1,),
            in_specs=[full(seg_rows.shape), head, head] + [full((2, block_rows, head_dim))] * block_count,
            out_specs=[head] + [full((block_rows, 2 * head_dim))] * block_count,
            scratch_shapes=[
                pltpu.VMEM((key_count, head_dim), jnp.bfloat16),
                pltpu.VMEM((head_dim, key_count), jnp.bfloat16),
                pltpu.VMEM((head_dim, key_count), jnp.bfloat16),
                pltpu.VMEM((row_count, key_count), jnp.int32),
                pltpu.VMEM((head_dim, key_count), jnp.float32),
                pltpu.VMEM((head_dim, key_count), jnp.float32),
            ],
        ),
        out_shape=[jax.ShapeDtypeStruct((row_count, width), jnp.bfloat16)] + [part] * block_count,
        compiler_params=pltpu.CompilerParams(dimension_semantics=("arbitrary",)),
    )(block_order, rank, seg_rows, query_states, out_grad, *kv_blocks)
    return outs[0], outs[1:]


def middle_kernel(block_count, head_dim, *refs):
    rank_ref, roll_ref, rows_ref = refs[:3]
    part_refs = refs[3 : 3 + block_count]
    kv_ref = refs[3 + block_count]
    out_refs = refs[4 + block_count :]
    total = part_refs[0][...].astype(jnp.float32)
    for b in range(1, block_count):
        total = total + part_refs[b][...].astype(jnp.float32)
    key_value = total.astype(jnp.bfloat16)
    kv_ref[...] = key_value
    key_grad = key_value[:, :head_dim]
    rank = rank_ref[0]
    for s in range(block_count):
        rows = rows_ref[(rank + s) % block_count]
        out_refs[s][...] = jnp.dot(rows, key_grad, preferred_element_type=jnp.float32).astype(jnp.bfloat16)


def key_value_and_products(rank, roll_rank, layer_input, part_blocks, roll_count, owner_rows):
    block_count = len(part_blocks)
    row_count, width = part_blocks[0].shape
    head_dim = width // 2
    features = layer_input.reshape(block_count, roll_count, owner_rows, row_count)
    full = lambda shape: pl.BlockSpec(shape, lambda i, *_: (0,) * len(shape))
    picked = pl.BlockSpec((block_count, None, owner_rows, row_count), lambda i, rank_ref, roll_ref: (0, roll_ref[0], 0, 0))
    product = jax.ShapeDtypeStruct((owner_rows, head_dim), jnp.bfloat16)
    outs = pl.pallas_call(
        functools.partial(middle_kernel, block_count, head_dim),
        grid_spec=pltpu.PrefetchScalarGridSpec(
            num_scalar_prefetch=2,
            grid=(1,),
            in_specs=[picked] + [full((row_count, width))] * block_count,
            out_specs=[full((row_count, width))] + [full((owner_rows, head_dim))] * block_count,
        ),
        out_shape=[jax.ShapeDtypeStruct((row_count, width), jnp.bfloat16)] + [product] * block_count,
    )(rank, roll_rank, features, *part_blocks)
    return outs[0], outs[1:]


def body(
    block_order,
    segment_ids,
    layer_input,
    query_states,
    key_states,
    value_states,
    out_grad,
    master_weight,
    first_moment,
    second_moment,
):
    row_count, head_dim = key_states.shape
    head_group = query_states.shape[1] // head_dim
    ctx_count = lax.axis_size("ctx")
    roll_count = lax.axis_size("roll")
    ctx_rank = lax.axis_index("ctx")
    roll_rank = lax.axis_index("roll")
    score_scale = head_dim ** (-0.5)

    seg_table = segment_ids.reshape(ctx_count, row_count)
    rank_vector = jnp.reshape(ctx_rank, (1,)).astype(jnp.int32)

    own_kv = jnp.stack([key_states, value_states])
    kv_blocks = [own_kv] + [
        shifted(own_kv, "ctx", ctx_count, -s) for s in range(1, ctx_count)
    ]
    query_grad, part_blocks = attention_backward(
        block_order,
        rank_vector,
        seg_table,
        query_states,
        out_grad,
        kv_blocks,
        head_dim,
        score_scale,
    )

    received = [part_blocks[0]] + [
        shifted(part_blocks[s], "ctx", ctx_count, s) for s in range(1, ctx_count)
    ]
    owner_rows = master_weight.shape[0]
    key_value, products = key_value_and_products(
        rank_vector,
        jnp.reshape(roll_rank, (1,)).astype(jnp.int32),
        layer_input,
        received,
        roll_count,
        owner_rows,
    )
    weight_grad = products[0].astype(jnp.float32)
    for s in range(1, ctx_count):
        weight_grad = weight_grad + shifted(products[s], "ctx", ctx_count, s).astype(jnp.float32)

    updated_first = BETA_ONE * first_moment + (1.0 - BETA_ONE) * weight_grad
    updated_second = BETA_TWO * second_moment + (1.0 - BETA_TWO) * weight_grad * weight_grad
    update = (
        updated_first / CORRECT_ONE / (jnp.sqrt(updated_second / CORRECT_TWO) + ADAM_EPS)
        + DECAY_RATE * master_weight
    )
    updated_master = master_weight - LEARN_RATE * update
    rollout_weight = lax.all_gather(updated_master.astype(jnp.bfloat16), "roll", axis=0, tiled=True)
    return (query_grad, key_value, updated_master, updated_first, updated_second, rollout_weight)


def solution(mesh):
    placed = (
        P(),
        P(),
        P(None, "ctx"),
        P("ctx", None),
        P("ctx", None),
        P("ctx", None),
        P("ctx", None),
        P(("ctx", "roll"), None),
        P(("ctx", "roll"), None),
        P(("ctx", "roll"), None),
    )
    return jax.shard_map(
        body,
        mesh=mesh,
        in_specs=placed,
        out_specs=(
            P("ctx", None),
            P("ctx", None),
            P(("ctx", "roll"), None),
            P(("ctx", "roll"), None),
            P(("ctx", "roll"), None),
            P("ctx", None),
        ),
        check_vma=False,
    )
```

```python
import functools

import jax
import jax.numpy as jnp
from jax import lax
from jax.experimental import pallas as pl
from jax.experimental.pallas import tpu as pltpu
from jax.sharding import PartitionSpec as P


NEG_FILL = -1e30
BETA_ONE = 0.9
BETA_TWO = 0.95
ADAM_EPS = 1e-08
DECAY_RATE = 0.1
LEARN_RATE = 1e-06
CORRECT_ONE = 0.9999734386011124
CORRECT_TWO = 0.994079470779666


def shifted(value, axis, count, shift):
    return lax.ppermute(value, axis, [(i, (i + shift) % count) for i in range(count)])


def attention_kernel(block_count, block_rows, head_dim, score_scale, *refs):
    order_ref, rank_ref, seg_ref, q_ref, do_ref, own_ref, mine_ref, other_ref = refs[:8]
    dq_ref = refs[8]
    part_refs = refs[9 : 9 + block_count]
    key_scr, kt_scr, vt_scr, mask_scr, dk_acc, dv_acc = refs[9 + block_count :]
    half = mine_ref.shape[0]
    low_is_mine = rank_ref[1] == 0

    def kv_block(b, which):
        if b == 0:
            return own_ref[which]
        if b <= half:
            return jnp.where(low_is_mine, mine_ref[b - 1, which], other_ref[b - 1, which])
        return jnp.where(low_is_mine, other_ref[b - 1 - half, which], mine_ref[b - 1 - half, which])

    step = pl.program_id(0)

    @pl.when(step == 0)
    def _():
        rank = rank_ref[0]
        lane = lax.broadcasted_iota(jnp.int32, (block_rows, block_rows), 1)
        sub = lax.broadcasted_iota(jnp.int32, (block_rows, block_rows), 0)
        own_seg = seg_ref[pl.ds(rank, 1), :]
        q_seg = jnp.sum(jnp.where(lane == sub, own_seg, 0), axis=1, keepdims=True)
        q_pos = order_ref[rank] * block_rows + sub[:, :1]
        for b in range(block_count):
            source = (rank + b) % block_count
            k_pos = order_ref[source] * block_rows + lane[:1, :]
            k_seg = seg_ref[pl.ds(source, 1), :]
            visible = (k_pos <= q_pos) & (k_seg == q_seg)
            cols = slice(b * block_rows, (b + 1) * block_rows)
            mask_scr[:, cols] = visible.astype(jnp.int32)
            key_block = kv_block(b, 0)
            key_scr[cols, :] = key_block
            kt_scr[:, cols] = key_block.astype(jnp.float32).T.astype(jnp.bfloat16)
            vt_scr[:, cols] = kv_block(b, 1).astype(jnp.float32).T.astype(jnp.bfloat16)
        dk_acc[...] = jnp.zeros_like(dk_acc)
        dv_acc[...] = jnp.zeros_like(dv_acc)

    head_count = q_ref.shape[1] // head_dim
    key_count = block_count * block_rows
    pair = max(
        g for g in range(1, head_count + 1)
        if head_count % g == 0 and g * q_ref.shape[0] * key_count <= 768 * 1024
    ) if q_ref.shape[0] * key_count <= 768 * 1024 else 1
    visible_rows = mask_scr[...] != 0
    visible = jnp.concatenate([visible_rows] * pair, axis=0) if pair > 1 else visible_rows
    for h in range(0, head_count, pair):
        head_cols = [slice((h + i) * head_dim, (h + i + 1) * head_dim) for i in range(pair)]
        q = jnp.concatenate([q_ref[:, c] for c in head_cols], axis=0) if pair > 1 else q_ref[:, head_cols[0]]
        do = jnp.concatenate([do_ref[:, c] for c in head_cols], axis=0) if pair > 1 else do_ref[:, head_cols[0]]
        scores = jnp.dot(q, kt_scr[...], preferred_element_type=jnp.float32) * score_scale
        scores = jnp.where(visible, scores, NEG_FILL)
        row_top = jnp.max(scores, axis=1, keepdims=True)
        expo = jnp.where(visible, jnp.exp(scores - row_top), 0.0)
        weights = expo * (1.0 / jnp.sum(expo, axis=1, keepdims=True))
        dprob = jnp.dot(do, vt_scr[...], preferred_element_type=jnp.float32)
        delta = jnp.sum(weights * dprob, axis=1, keepdims=True)
        dscore = weights * (dprob - delta)
        weights_half = weights.astype(jnp.bfloat16)
        dscore_half = dscore.astype(jnp.bfloat16)
        query_part = jnp.dot(dscore_half, key_scr[...], preferred_element_type=jnp.float32) * score_scale
        rows = query_part.shape[0] // pair
        for i, c in enumerate(head_cols):
            dq_ref[:, c] = query_part[i * rows : (i + 1) * rows].astype(dq_ref.dtype)
        q_t = q.astype(jnp.float32).T.astype(jnp.bfloat16)
        do_t = do.astype(jnp.float32).T.astype(jnp.bfloat16)
        dk_acc[...] += jnp.dot(q_t, dscore_half, preferred_element_type=jnp.float32)
        dv_acc[...] += jnp.dot(do_t, weights_half, preferred_element_type=jnp.float32)

    @pl.when(step == pl.num_programs(0) - 1)
    def _():
        for b in range(block_count):
            cols = slice(b * block_rows, (b + 1) * block_rows)
            part_refs[b][:, :head_dim] = (dk_acc[:, cols].T * score_scale).astype(jnp.bfloat16)
            part_refs[b][:, head_dim:] = dv_acc[:, cols].T.astype(jnp.bfloat16)


def attention_backward(block_order, rank, seg_rows, query_states, out_grad, own_kv, mine, other, head_dim, score_scale):
    row_count, width = query_states.shape
    head_group = width // head_dim
    block_count = seg_rows.shape[0]
    block_rows = own_kv.shape[1]
    key_count = block_count * block_rows
    full = lambda shape: pl.BlockSpec(shape, lambda h, *_: (0,) * len(shape))
    head = pl.BlockSpec((row_count, width), lambda h, *_: (0, 0))
    part = jax.ShapeDtypeStruct((block_rows, 2 * head_dim), jnp.bfloat16)
    kernel = functools.partial(attention_kernel, block_count, block_rows, head_dim, score_scale)
    outs = pl.pallas_call(
        kernel,
        grid_spec=pltpu.PrefetchScalarGridSpec(
            num_scalar_prefetch=2,
            grid=(1,),
            in_specs=[full(seg_rows.shape), head, head, full(own_kv.shape), full(mine.shape), full(other.shape)],
            out_specs=[head] + [full((block_rows, 2 * head_dim))] * block_count,
            scratch_shapes=[
                pltpu.VMEM((key_count, head_dim), jnp.bfloat16),
                pltpu.VMEM((head_dim, key_count), jnp.bfloat16),
                pltpu.VMEM((head_dim, key_count), jnp.bfloat16),
                pltpu.VMEM((row_count, key_count), jnp.int32),
                pltpu.VMEM((head_dim, key_count), jnp.float32),
                pltpu.VMEM((head_dim, key_count), jnp.float32),
            ],
        ),
        out_shape=[jax.ShapeDtypeStruct((row_count, width), jnp.bfloat16)] + [part] * block_count,
        compiler_params=pltpu.CompilerParams(dimension_semantics=("arbitrary",)),
    )(block_order, rank, seg_rows, query_states, out_grad, own_kv, mine, other)
    return outs[0], outs[1:]


def middle_kernel(block_count, head_dim, *refs):
    rank_ref, roll_ref, rows_ref = refs[:3]
    part_refs = refs[3 : 3 + block_count]
    kv_ref = refs[3 + block_count]
    out_refs = refs[4 + block_count :]
    total = part_refs[0][...].astype(jnp.float32)
    for b in range(1, block_count):
        total = total + part_refs[b][...].astype(jnp.float32)
    key_value = total.astype(jnp.bfloat16)
    kv_ref[...] = key_value
    key_grad = key_value[:, :head_dim]
    rank = rank_ref[0]
    for s in range(block_count):
        rows = rows_ref[(rank + s) % block_count]
        out_refs[s][...] = jnp.dot(rows, key_grad, preferred_element_type=jnp.float32).astype(jnp.bfloat16)


def key_value_and_products(rank, roll_rank, layer_input, part_blocks, roll_count, owner_rows):
    block_count = len(part_blocks)
    row_count, width = part_blocks[0].shape
    head_dim = width // 2
    features = layer_input.reshape(block_count, roll_count, owner_rows, row_count)
    full = lambda shape: pl.BlockSpec(shape, lambda i, *_: (0,) * len(shape))
    picked = pl.BlockSpec((block_count, None, owner_rows, row_count), lambda i, rank_ref, roll_ref: (0, roll_ref[0], 0, 0))
    product = jax.ShapeDtypeStruct((owner_rows, head_dim), jnp.bfloat16)
    outs = pl.pallas_call(
        functools.partial(middle_kernel, block_count, head_dim),
        grid_spec=pltpu.PrefetchScalarGridSpec(
            num_scalar_prefetch=2,
            grid=(1,),
            in_specs=[picked] + [full((row_count, width))] * block_count,
            out_specs=[full((row_count, width))] + [full((owner_rows, head_dim))] * block_count,
        ),
        out_shape=[jax.ShapeDtypeStruct((row_count, width), jnp.bfloat16)] + [product] * block_count,
    )(rank, roll_rank, features, *part_blocks)
    return outs[0], outs[1:]


def body(
    block_order,
    segment_ids,
    layer_input,
    query_states,
    key_states,
    value_states,
    out_grad,
    master_weight,
    first_moment,
    second_moment,
):
    row_count, head_dim = key_states.shape
    head_group = query_states.shape[1] // head_dim
    ctx_count = lax.axis_size("ctx")
    roll_count = lax.axis_size("roll")
    ctx_rank = lax.axis_index("ctx")
    roll_rank = lax.axis_index("roll")
    score_scale = head_dim ** (-0.5)

    seg_table = segment_ids.reshape(ctx_count, row_count)
    rank_vector = jnp.reshape(ctx_rank, (1,)).astype(jnp.int32)

    own_kv = jnp.stack([key_states, value_states])
    half = ctx_count // 2
    fetched = []
    for k in range(half):
        pairs = []
        for c in range(ctx_count):
            for r in range(roll_count):
                s = 1 + k + half * (r % 2)
                if s < ctx_count:
                    pairs.append((c * roll_count + r, ((c - s) % ctx_count) * roll_count + r))
        fetched.append(lax.ppermute(own_kv, ("ctx", "roll"), pairs))
    mine = jnp.stack(fetched)
    other = lax.ppermute(mine, "roll", [(r, r ^ 1) for r in range(roll_count)])
    core_rank = jnp.stack([ctx_rank, roll_rank % 2]).astype(jnp.int32)
    query_grad, part_blocks = attention_backward(
        block_order,
        core_rank,
        seg_table,
        query_states,
        out_grad,
        own_kv,
        mine,
        other,
        head_dim,
        score_scale,
    )

    received = [part_blocks[0]] + [
        shifted(part_blocks[s], "ctx", ctx_count, s) for s in range(1, ctx_count)
    ]
    owner_rows = master_weight.shape[0]
    key_value, products = key_value_and_products(
        rank_vector,
        jnp.reshape(roll_rank, (1,)).astype(jnp.int32),
        layer_input,
        received,
        roll_count,
        owner_rows,
    )
    weight_grad = products[0].astype(jnp.float32)
    for s in range(1, ctx_count):
        weight_grad = weight_grad + shifted(products[s], "ctx", ctx_count, s).astype(jnp.float32)

    updated_first = BETA_ONE * first_moment + (1.0 - BETA_ONE) * weight_grad
    updated_second = BETA_TWO * second_moment + (1.0 - BETA_TWO) * weight_grad * weight_grad
    update = (
        updated_first / CORRECT_ONE / (jnp.sqrt(updated_second / CORRECT_TWO) + ADAM_EPS)
        + DECAY_RATE * master_weight
    )
    updated_master = master_weight - LEARN_RATE * update
    rollout_weight = lax.all_gather(updated_master.astype(jnp.bfloat16), "roll", axis=0, tiled=True)
    return (query_grad, key_value, updated_master, updated_first, updated_second, rollout_weight)


def solution(mesh):
    placed = (
        P(),
        P(),
        P(None, "ctx"),
        P("ctx", None),
        P("ctx", None),
        P("ctx", None),
        P("ctx", None),
        P(("ctx", "roll"), None),
        P(("ctx", "roll"), None),
        P(("ctx", "roll"), None),
    )
    return jax.shard_map(
        body,
        mesh=mesh,
        in_specs=placed,
        out_specs=(
            P("ctx", None),
            P("ctx", None),
            P(("ctx", "roll"), None),
            P(("ctx", "roll"), None),
            P(("ctx", "roll"), None),
            P("ctx", None),
        ),
        check_vma=False,
    )
```

```python
import functools

import jax
import jax.numpy as jnp
from jax import lax
from jax.experimental import pallas as pl
from jax.experimental.pallas import tpu as pltpu
from jax.sharding import PartitionSpec as P


NEG_FILL = -1e30
BETA_ONE = 0.9
BETA_TWO = 0.95
ADAM_EPS = 1e-08
DECAY_RATE = 0.1
LEARN_RATE = 1e-06
CORRECT_ONE = 0.9999734386011124
CORRECT_TWO = 0.994079470779666


def shifted(value, axis, count, shift):
    return lax.ppermute(value, axis, [(i, (i + shift) % count) for i in range(count)])


def attention_kernel(block_count, block_rows, head_dim, score_scale, *refs):
    order_ref, rank_ref, seg_ref, q_ref, do_ref, own_ref, mine_ref, other_ref = refs[:8]
    half = mine_ref.shape[0]
    dq_ref = refs[8]
    part_refs = refs[9 : 10 + half]
    key_scr, kt_scr, vt_scr, mask_scr, dk_acc, dv_acc = refs[10 + half :]
    low_is_mine = rank_ref[1] == 0

    def kv_block(b, which):
        if b == 0:
            return own_ref[which]
        if b <= half:
            return jnp.where(low_is_mine, mine_ref[b - 1, which], other_ref[b - 1, which])
        return jnp.where(low_is_mine, other_ref[b - 1 - half, which], mine_ref[b - 1 - half, which])

    step = pl.program_id(0)

    @pl.when(step == 0)
    def _():
        rank = rank_ref[0]
        lane = lax.broadcasted_iota(jnp.int32, (block_rows, block_rows), 1)
        sub = lax.broadcasted_iota(jnp.int32, (block_rows, block_rows), 0)
        own_seg = seg_ref[pl.ds(rank, 1), :]
        q_seg = jnp.sum(jnp.where(lane == sub, own_seg, 0), axis=1, keepdims=True)
        q_pos = order_ref[rank] * block_rows + sub[:, :1]
        for b in range(block_count):
            source = (rank + b) % block_count
            k_pos = order_ref[source] * block_rows + lane[:1, :]
            k_seg = seg_ref[pl.ds(source, 1), :]
            visible = (k_pos <= q_pos) & (k_seg == q_seg)
            cols = slice(b * block_rows, (b + 1) * block_rows)
            mask_scr[:, cols] = visible.astype(jnp.int32)
            key_block = kv_block(b, 0)
            key_scr[cols, :] = key_block
            kt_scr[:, cols] = key_block.astype(jnp.float32).T.astype(jnp.bfloat16)
            vt_scr[:, cols] = kv_block(b, 1).astype(jnp.float32).T.astype(jnp.bfloat16)
        dk_acc[...] = jnp.zeros_like(dk_acc)
        dv_acc[...] = jnp.zeros_like(dv_acc)

    head_count = q_ref.shape[1] // head_dim
    key_count = block_count * block_rows
    pair = max(
        g for g in range(1, head_count + 1)
        if head_count % g == 0 and g * q_ref.shape[0] * key_count <= 768 * 1024
    ) if q_ref.shape[0] * key_count <= 768 * 1024 else 1
    visible_rows = mask_scr[...] != 0
    visible = jnp.concatenate([visible_rows] * pair, axis=0) if pair > 1 else visible_rows
    for h in range(0, head_count, pair):
        head_cols = [slice((h + i) * head_dim, (h + i + 1) * head_dim) for i in range(pair)]
        q = jnp.concatenate([q_ref[:, c] for c in head_cols], axis=0) if pair > 1 else q_ref[:, head_cols[0]]
        do = jnp.concatenate([do_ref[:, c] for c in head_cols], axis=0) if pair > 1 else do_ref[:, head_cols[0]]
        scores = jnp.dot(q, kt_scr[...], preferred_element_type=jnp.float32) * score_scale
        scores = jnp.where(visible, scores, NEG_FILL)
        row_top = jnp.max(scores, axis=1, keepdims=True)
        expo = jnp.where(visible, jnp.exp(scores - row_top), 0.0)
        weights = expo * (1.0 / jnp.sum(expo, axis=1, keepdims=True))
        dprob = jnp.dot(do, vt_scr[...], preferred_element_type=jnp.float32)
        delta = jnp.sum(weights * dprob, axis=1, keepdims=True)
        dscore = weights * (dprob - delta)
        weights_half = weights.astype(jnp.bfloat16)
        dscore_half = dscore.astype(jnp.bfloat16)
        query_part = jnp.dot(dscore_half, key_scr[...], preferred_element_type=jnp.float32) * score_scale
        rows = query_part.shape[0] // pair
        for i, c in enumerate(head_cols):
            dq_ref[:, c] = query_part[i * rows : (i + 1) * rows].astype(dq_ref.dtype)
        q_t = q.astype(jnp.float32).T.astype(jnp.bfloat16)
        do_t = do.astype(jnp.float32).T.astype(jnp.bfloat16)
        dk_acc[...] += jnp.dot(q_t, dscore_half, preferred_element_type=jnp.float32)
        dv_acc[...] += jnp.dot(do_t, weights_half, preferred_element_type=jnp.float32)

    @pl.when(step == pl.num_programs(0) - 1)
    def _():
        def part_of(b):
            cols = slice(b * block_rows, (b + 1) * block_rows)
            key_part = (dk_acc[:, cols].T * score_scale).astype(jnp.bfloat16)
            value_part = dv_acc[:, cols].T.astype(jnp.bfloat16)
            return key_part, value_part

        own_key, own_value = part_of(0)
        part_refs[0][:, :head_dim] = own_key
        part_refs[0][:, head_dim:] = own_value
        for k in range(half):
            low_key, low_value = part_of(1 + k)
            if 1 + k + half < block_count:
                high_key, high_value = part_of(1 + k + half)
                low_key = jnp.where(low_is_mine, low_key, high_key)
                low_value = jnp.where(low_is_mine, low_value, high_value)
            part_refs[1 + k][:, :head_dim] = low_key
            part_refs[1 + k][:, head_dim:] = low_value


def attention_backward(block_order, rank, seg_rows, query_states, out_grad, own_kv, mine, other, head_dim, score_scale):
    row_count, width = query_states.shape
    head_group = width // head_dim
    block_count = seg_rows.shape[0]
    block_rows = own_kv.shape[1]
    key_count = block_count * block_rows
    full = lambda shape: pl.BlockSpec(shape, lambda h, *_: (0,) * len(shape))
    head = pl.BlockSpec((row_count, width), lambda h, *_: (0, 0))
    part = jax.ShapeDtypeStruct((block_rows, 2 * head_dim), jnp.bfloat16)
    kernel = functools.partial(attention_kernel, block_count, block_rows, head_dim, score_scale)
    outs = pl.pallas_call(
        kernel,
        grid_spec=pltpu.PrefetchScalarGridSpec(
            num_scalar_prefetch=2,
            grid=(1,),
            in_specs=[full(seg_rows.shape), head, head, full(own_kv.shape), full(mine.shape), full(other.shape)],
            out_specs=[head] + [full((block_rows, 2 * head_dim))] * (1 + mine.shape[0]),
            scratch_shapes=[
                pltpu.VMEM((key_count, head_dim), jnp.bfloat16),
                pltpu.VMEM((head_dim, key_count), jnp.bfloat16),
                pltpu.VMEM((head_dim, key_count), jnp.bfloat16),
                pltpu.VMEM((row_count, key_count), jnp.int32),
                pltpu.VMEM((head_dim, key_count), jnp.float32),
                pltpu.VMEM((head_dim, key_count), jnp.float32),
            ],
        ),
        out_shape=[jax.ShapeDtypeStruct((row_count, width), jnp.bfloat16)] + [part] * (1 + mine.shape[0]),
        compiler_params=pltpu.CompilerParams(dimension_semantics=("arbitrary",)),
    )(block_order, rank, seg_rows, query_states, out_grad, own_kv, mine, other)
    return outs[0], outs[1:]


def middle_kernel(block_count, head_dim, *refs):
    rank_ref, roll_ref, rows_ref, own_ref, mine_ref, other_ref, kv_ref = refs[:7]
    out_refs = refs[7:]
    low_is_mine = roll_ref[0] % 2 == 0
    low = jnp.where(low_is_mine, mine_ref[...], other_ref[...])
    high = jnp.where(low_is_mine, other_ref[...], mine_ref[...])
    total = own_ref[...].astype(jnp.float32) + low + high
    key_value = total.astype(jnp.bfloat16)
    kv_ref[...] = key_value
    key_grad = key_value[:, :head_dim]
    rank = rank_ref[0]
    for s in range(block_count):
        rows = rows_ref[(rank + s) % block_count]
        out_refs[s][...] = jnp.dot(rows, key_grad, preferred_element_type=jnp.float32).astype(jnp.bfloat16)


def key_value_and_products(rank, roll_rank, layer_input, own_part, mine, other, roll_count, owner_rows):
    block_count = layer_input.shape[0] // (roll_count * owner_rows)
    row_count, width = own_part.shape
    head_dim = width // 2
    features = layer_input.reshape(block_count, roll_count, owner_rows, row_count)
    full = lambda shape: pl.BlockSpec(shape, lambda i, *_: (0,) * len(shape))
    picked = pl.BlockSpec((block_count, None, owner_rows, row_count), lambda i, rank_ref, roll_ref: (0, roll_ref[0], 0, 0))
    product = jax.ShapeDtypeStruct((owner_rows, head_dim), jnp.bfloat16)
    outs = pl.pallas_call(
        functools.partial(middle_kernel, block_count, head_dim),
        grid_spec=pltpu.PrefetchScalarGridSpec(
            num_scalar_prefetch=2,
            grid=(1,),
            in_specs=[picked] + [full((row_count, width))] * 3,
            out_specs=[full((row_count, width))] + [full((owner_rows, head_dim))] * block_count,
        ),
        out_shape=[jax.ShapeDtypeStruct((row_count, width), jnp.bfloat16)] + [product] * block_count,
    )(rank, roll_rank, features, own_part, mine, other)
    return outs[0], outs[1:]


def body(
    block_order,
    segment_ids,
    layer_input,
    query_states,
    key_states,
    value_states,
    out_grad,
    master_weight,
    first_moment,
    second_moment,
):
    row_count, head_dim = key_states.shape
    head_group = query_states.shape[1] // head_dim
    ctx_count = lax.axis_size("ctx")
    roll_count = lax.axis_size("roll")
    ctx_rank = lax.axis_index("ctx")
    roll_rank = lax.axis_index("roll")
    score_scale = head_dim ** (-0.5)

    seg_table = segment_ids.reshape(ctx_count, row_count)
    rank_vector = jnp.reshape(ctx_rank, (1,)).astype(jnp.int32)

    own_kv = jnp.stack([key_states, value_states])
    half = ctx_count // 2
    fetched = []
    for k in range(half):
        pairs = []
        for c in range(ctx_count):
            for r in range(roll_count):
                s = 1 + k + half * (r % 2)
                if s < ctx_count:
                    pairs.append((c * roll_count + r, ((c - s) % ctx_count) * roll_count + r))
        fetched.append(lax.ppermute(own_kv, ("ctx", "roll"), pairs))
    mine = jnp.stack(fetched)
    other = lax.ppermute(mine, "roll", [(r, r ^ 1) for r in range(roll_count)])
    core_rank = jnp.stack([ctx_rank, roll_rank % 2]).astype(jnp.int32)
    query_grad, part_blocks = attention_backward(
        block_order,
        core_rank,
        seg_table,
        query_states,
        out_grad,
        own_kv,
        mine,
        other,
        head_dim,
        score_scale,
    )

    mine_sum = None
    for k in range(half):
        pairs = []
        for c in range(ctx_count):
            for r in range(roll_count):
                s = 1 + k + half * (r % 2)
                if s < ctx_count:
                    pairs.append((c * roll_count + r, ((c + s) % ctx_count) * roll_count + r))
        arrived = lax.ppermute(part_blocks[1 + k], ("ctx", "roll"), pairs).astype(jnp.float32)
        mine_sum = arrived if mine_sum is None else mine_sum + arrived
    other_sum = lax.ppermute(mine_sum, "roll", [(r, r ^ 1) for r in range(roll_count)])
    owner_rows = master_weight.shape[0]
    key_value, products = key_value_and_products(
        rank_vector,
        jnp.reshape(roll_rank, (1,)).astype(jnp.int32),
        layer_input,
        part_blocks[0],
        mine_sum,
        other_sum,
        roll_count,
        owner_rows,
    )
    weight_grad = products[0].astype(jnp.float32)
    for s in range(1, ctx_count):
        weight_grad = weight_grad + shifted(products[s], "ctx", ctx_count, s).astype(jnp.float32)

    updated_first = BETA_ONE * first_moment + (1.0 - BETA_ONE) * weight_grad
    updated_second = BETA_TWO * second_moment + (1.0 - BETA_TWO) * weight_grad * weight_grad
    update = (
        updated_first / CORRECT_ONE / (jnp.sqrt(updated_second / CORRECT_TWO) + ADAM_EPS)
        + DECAY_RATE * master_weight
    )
    updated_master = master_weight - LEARN_RATE * update
    rollout_weight = lax.all_gather(updated_master.astype(jnp.bfloat16), "roll", axis=0, tiled=True)
    return (query_grad, key_value, updated_master, updated_first, updated_second, rollout_weight)


def solution(mesh):
    placed = (
        P(),
        P(),
        P(None, "ctx"),
        P("ctx", None),
        P("ctx", None),
        P("ctx", None),
        P("ctx", None),
        P(("ctx", "roll"), None),
        P(("ctx", "roll"), None),
        P(("ctx", "roll"), None),
    )
    return jax.shard_map(
        body,
        mesh=mesh,
        in_specs=placed,
        out_specs=(
            P("ctx", None),
            P("ctx", None),
            P(("ctx", "roll"), None),
            P(("ctx", "roll"), None),
            P(("ctx", "roll"), None),
            P("ctx", None),
        ),
        check_vma=False,
    )
```

```python
import functools

import jax
import jax.numpy as jnp
from jax import lax
from jax.experimental import pallas as pl
from jax.experimental.pallas import tpu as pltpu
from jax.sharding import PartitionSpec as P


NEG_FILL = -1e30
BETA_ONE = 0.9
BETA_TWO = 0.95
ADAM_EPS = 1e-08
DECAY_RATE = 0.1
LEARN_RATE = 1e-06
CORRECT_ONE = 0.9999734386011124
CORRECT_TWO = 0.994079470779666


def shifted(value, axis, count, shift):
    return lax.ppermute(value, axis, [(i, (i + shift) % count) for i in range(count)])


def attention_kernel(block_count, block_rows, head_dim, score_scale, *refs):
    order_ref, rank_ref, seg_ref, q_ref, do_ref, own_ref, mine_ref, other_ref = refs[:8]
    half = mine_ref.shape[0]
    dq_ref = refs[8]
    part_refs = refs[9 : 10 + half]
    key_scr, kt_scr, vt_scr, mask_scr, dk_acc, dv_acc = refs[10 + half :]
    low_is_mine = rank_ref[1] == 0

    def kv_block(b, which):
        if b == 0:
            return own_ref[which]
        if b <= half:
            return jnp.where(low_is_mine, mine_ref[b - 1, which], other_ref[b - 1, which])
        return jnp.where(low_is_mine, other_ref[b - 1 - half, which], mine_ref[b - 1 - half, which])

    step = pl.program_id(0)

    @pl.when(step == 0)
    def _():
        rank = rank_ref[0]
        lane = lax.broadcasted_iota(jnp.int32, (block_rows, block_rows), 1)
        sub = lax.broadcasted_iota(jnp.int32, (block_rows, block_rows), 0)
        own_seg = seg_ref[pl.ds(rank, 1), :]
        q_seg = jnp.sum(jnp.where(lane == sub, own_seg, 0), axis=1, keepdims=True)
        q_pos = order_ref[rank] * block_rows + sub[:, :1]
        for b in range(block_count):
            source = (rank + b) % block_count
            k_pos = order_ref[source] * block_rows + lane[:1, :]
            k_seg = seg_ref[pl.ds(source, 1), :]
            visible = (k_pos <= q_pos) & (k_seg == q_seg)
            cols = slice(b * block_rows, (b + 1) * block_rows)
            mask_scr[:, cols] = visible.astype(jnp.int32)
            key_block = kv_block(b, 0)
            key_scr[cols, :] = key_block
            kt_scr[:, cols] = key_block.astype(jnp.float32).T.astype(jnp.bfloat16)
            vt_scr[:, cols] = kv_block(b, 1).astype(jnp.float32).T.astype(jnp.bfloat16)
        dk_acc[...] = jnp.zeros_like(dk_acc)
        dv_acc[...] = jnp.zeros_like(dv_acc)

    head_count = q_ref.shape[1] // head_dim
    key_count = block_count * block_rows
    pair = max(
        g for g in range(1, head_count + 1)
        if head_count % g == 0 and g * q_ref.shape[0] * key_count <= 768 * 1024
    ) if q_ref.shape[0] * key_count <= 768 * 1024 else 1
    visible_rows = mask_scr[...] != 0
    visible = jnp.concatenate([visible_rows] * pair, axis=0) if pair > 1 else visible_rows
    for h in range(0, head_count, pair):
        head_cols = [slice((h + i) * head_dim, (h + i + 1) * head_dim) for i in range(pair)]
        q = jnp.concatenate([q_ref[:, c] for c in head_cols], axis=0) if pair > 1 else q_ref[:, head_cols[0]]
        do = jnp.concatenate([do_ref[:, c] for c in head_cols], axis=0) if pair > 1 else do_ref[:, head_cols[0]]
        scores = jnp.dot(q, kt_scr[...], preferred_element_type=jnp.float32) * score_scale
        scores = jnp.where(visible, scores, NEG_FILL)
        row_top = jnp.max(scores, axis=1, keepdims=True)
        expo = jnp.where(visible, jnp.exp(scores - row_top), 0.0)
        weights = expo * (1.0 / jnp.sum(expo, axis=1, keepdims=True))
        dprob = jnp.dot(do, vt_scr[...], preferred_element_type=jnp.float32)
        delta = jnp.sum(weights * dprob, axis=1, keepdims=True)
        dscore = weights * (dprob - delta)
        weights_half = weights.astype(jnp.bfloat16)
        dscore_half = dscore.astype(jnp.bfloat16)
        query_part = jnp.dot(dscore_half, key_scr[...], preferred_element_type=jnp.float32) * score_scale
        rows = query_part.shape[0] // pair
        for i, c in enumerate(head_cols):
            dq_ref[:, c] = query_part[i * rows : (i + 1) * rows].astype(dq_ref.dtype)
        q_t = q.astype(jnp.float32).T.astype(jnp.bfloat16)
        do_t = do.astype(jnp.float32).T.astype(jnp.bfloat16)
        dk_acc[...] += jnp.dot(q_t, dscore_half, preferred_element_type=jnp.float32)
        dv_acc[...] += jnp.dot(do_t, weights_half, preferred_element_type=jnp.float32)

    @pl.when(step == pl.num_programs(0) - 1)
    def _():
        def part_of(b):
            cols = slice(b * block_rows, (b + 1) * block_rows)
            key_part = (dk_acc[:, cols].T * score_scale).astype(jnp.bfloat16)
            value_part = dv_acc[:, cols].T.astype(jnp.bfloat16)
            return key_part, value_part

        own_key, own_value = part_of(0)
        part_refs[0][:, :head_dim] = own_key
        part_refs[0][:, head_dim:] = own_value
        for k in range(half):
            low_key, low_value = part_of(1 + k)
            if 1 + k + half < block_count:
                high_key, high_value = part_of(1 + k + half)
                low_key = jnp.where(low_is_mine, low_key, high_key)
                low_value = jnp.where(low_is_mine, low_value, high_value)
            part_refs[1 + k][:, :head_dim] = low_key
            part_refs[1 + k][:, head_dim:] = low_value


def attention_backward(block_order, rank, seg_rows, query_states, out_grad, own_kv, mine, other, head_dim, score_scale):
    row_count, width = query_states.shape
    head_group = width // head_dim
    block_count = seg_rows.shape[0]
    block_rows = own_kv.shape[1]
    key_count = block_count * block_rows
    full = lambda shape: pl.BlockSpec(shape, lambda h, *_: (0,) * len(shape))
    head = pl.BlockSpec((row_count, width), lambda h, *_: (0, 0))
    part = jax.ShapeDtypeStruct((block_rows, 2 * head_dim), jnp.bfloat16)
    kernel = functools.partial(attention_kernel, block_count, block_rows, head_dim, score_scale)
    outs = pl.pallas_call(
        kernel,
        grid_spec=pltpu.PrefetchScalarGridSpec(
            num_scalar_prefetch=2,
            grid=(1,),
            in_specs=[full(seg_rows.shape), head, head, full(own_kv.shape), full(mine.shape), full(other.shape)],
            out_specs=[head] + [full((block_rows, 2 * head_dim))] * (1 + mine.shape[0]),
            scratch_shapes=[
                pltpu.VMEM((key_count, head_dim), jnp.bfloat16),
                pltpu.VMEM((head_dim, key_count), jnp.bfloat16),
                pltpu.VMEM((head_dim, key_count), jnp.bfloat16),
                pltpu.VMEM((row_count, key_count), jnp.int32),
                pltpu.VMEM((head_dim, key_count), jnp.float32),
                pltpu.VMEM((head_dim, key_count), jnp.float32),
            ],
        ),
        out_shape=[jax.ShapeDtypeStruct((row_count, width), jnp.bfloat16)] + [part] * (1 + mine.shape[0]),
        compiler_params=pltpu.CompilerParams(dimension_semantics=("arbitrary",)),
    )(block_order, rank, seg_rows, query_states, out_grad, own_kv, mine, other)
    return outs[0], outs[1:]


def middle_kernel(block_count, head_dim, *refs):
    rank_ref, roll_ref, rows_ref, own_ref, mine_ref, other_ref, kv_ref = refs[:7]
    out_refs = refs[7:]
    low_is_mine = roll_ref[0] % 2 == 0
    low = jnp.where(low_is_mine, mine_ref[...], other_ref[...])
    high = jnp.where(low_is_mine, other_ref[...], mine_ref[...])
    total = own_ref[...].astype(jnp.float32) + low + high
    key_value = total.astype(jnp.bfloat16)
    kv_ref[...] = key_value
    key_grad = key_value[:, :head_dim]
    rank = rank_ref[0]
    parity = roll_ref[0] % 2
    half = len(out_refs) - 1

    def product(target, which):
        rows = rows_ref[target, which]
        return jnp.dot(rows, key_grad, preferred_element_type=jnp.float32).astype(jnp.bfloat16)

    out_refs[0][...] = jnp.where(parity == 0, product(rank, 0), product(rank, 1))
    for k in range(half):
        shift = 1 + k + half * parity
        target = (rank + shift) % block_count
        out_refs[1 + k][0] = product(target, 0)
        out_refs[1 + k][1] = product(target, 1)


def key_value_and_products(rank, roll_rank, layer_input, own_part, mine, other, roll_count, owner_rows):
    block_count = layer_input.shape[0] // (roll_count * owner_rows)
    row_count, width = own_part.shape
    head_dim = width // 2
    features = layer_input.reshape(block_count, roll_count, owner_rows, row_count)
    full = lambda shape: pl.BlockSpec(shape, lambda i, *_: (0,) * len(shape))
    picked = pl.BlockSpec((block_count, 2, owner_rows, row_count), lambda i, rank_ref, roll_ref: (0, roll_ref[0] // 2, 0, 0))
    half = block_count // 2
    own = jax.ShapeDtypeStruct((owner_rows, head_dim), jnp.bfloat16)
    both = jax.ShapeDtypeStruct((2, owner_rows, head_dim), jnp.bfloat16)
    outs = pl.pallas_call(
        functools.partial(middle_kernel, block_count, head_dim),
        grid_spec=pltpu.PrefetchScalarGridSpec(
            num_scalar_prefetch=2,
            grid=(1,),
            in_specs=[picked] + [full((row_count, width))] * 3,
            out_specs=[full((row_count, width)), full((owner_rows, head_dim))]
            + [full((2, owner_rows, head_dim))] * half,
        ),
        out_shape=[jax.ShapeDtypeStruct((row_count, width), jnp.bfloat16), own] + [both] * half,
    )(rank, roll_rank, features, own_part, mine, other)
    return outs[0], outs[1:]


def body(
    block_order,
    segment_ids,
    layer_input,
    query_states,
    key_states,
    value_states,
    out_grad,
    master_weight,
    first_moment,
    second_moment,
):
    row_count, head_dim = key_states.shape
    head_group = query_states.shape[1] // head_dim
    ctx_count = lax.axis_size("ctx")
    roll_count = lax.axis_size("roll")
    ctx_rank = lax.axis_index("ctx")
    roll_rank = lax.axis_index("roll")
    score_scale = head_dim ** (-0.5)

    seg_table = segment_ids.reshape(ctx_count, row_count)
    rank_vector = jnp.reshape(ctx_rank, (1,)).astype(jnp.int32)

    own_kv = jnp.stack([key_states, value_states])
    half = ctx_count // 2
    fetched = []
    for k in range(half):
        pairs = []
        for c in range(ctx_count):
            for r in range(roll_count):
                s = 1 + k + half * (r % 2)
                if s < ctx_count:
                    pairs.append((c * roll_count + r, ((c - s) % ctx_count) * roll_count + r))
        fetched.append(lax.ppermute(own_kv, ("ctx", "roll"), pairs))
    mine = jnp.stack(fetched)
    other = lax.ppermute(mine, "roll", [(r, r ^ 1) for r in range(roll_count)])
    core_rank = jnp.stack([ctx_rank, roll_rank % 2]).astype(jnp.int32)
    query_grad, part_blocks = attention_backward(
        block_order,
        core_rank,
        seg_table,
        query_states,
        out_grad,
        own_kv,
        mine,
        other,
        head_dim,
        score_scale,
    )

    mine_sum = None
    for k in range(half):
        pairs = []
        for c in range(ctx_count):
            for r in range(roll_count):
                s = 1 + k + half * (r % 2)
                if s < ctx_count:
                    pairs.append((c * roll_count + r, ((c + s) % ctx_count) * roll_count + r))
        arrived = lax.ppermute(part_blocks[1 + k], ("ctx", "roll"), pairs).astype(jnp.float32)
        mine_sum = arrived if mine_sum is None else mine_sum + arrived
    other_sum = lax.ppermute(mine_sum, "roll", [(r, r ^ 1) for r in range(roll_count)])
    owner_rows = master_weight.shape[0]
    key_value, products = key_value_and_products(
        rank_vector,
        jnp.reshape(roll_rank, (1,)).astype(jnp.int32),
        layer_input,
        part_blocks[0],
        mine_sum,
        other_sum,
        roll_count,
        owner_rows,
    )
    pair_sum = None
    for k in range(half):
        pairs = []
        for c in range(ctx_count):
            for r in range(roll_count):
                s = 1 + k + half * (r % 2)
                if s < ctx_count:
                    pairs.append((c * roll_count + r, ((c + s) % ctx_count) * roll_count + r))
        arrived = lax.ppermute(products[1 + k], ("ctx", "roll"), pairs).astype(jnp.float32)
        pair_sum = arrived if pair_sum is None else pair_sum + arrived
    parity = roll_rank % 2
    mine_rows = lax.dynamic_index_in_dim(pair_sum, parity, 0, keepdims=False)
    partner_rows = lax.dynamic_index_in_dim(pair_sum, 1 - parity, 0, keepdims=False)
    from_partner = lax.ppermute(partner_rows, "roll", [(r, r ^ 1) for r in range(roll_count)])
    low = jnp.where(parity == 0, mine_rows, from_partner)
    high = jnp.where(parity == 0, from_partner, mine_rows)
    weight_grad = products[0].astype(jnp.float32) + low + high

    updated_first = BETA_ONE * first_moment + (1.0 - BETA_ONE) * weight_grad
    updated_second = BETA_TWO * second_moment + (1.0 - BETA_TWO) * weight_grad * weight_grad
    update = (
        updated_first / CORRECT_ONE / (jnp.sqrt(updated_second / CORRECT_TWO) + ADAM_EPS)
        + DECAY_RATE * master_weight
    )
    updated_master = master_weight - LEARN_RATE * update
    rollout_weight = lax.all_gather(updated_master.astype(jnp.bfloat16), "roll", axis=0, tiled=True)
    return (query_grad, key_value, updated_master, updated_first, updated_second, rollout_weight)


def solution(mesh):
    placed = (
        P(),
        P(),
        P(None, "ctx"),
        P("ctx", None),
        P("ctx", None),
        P("ctx", None),
        P("ctx", None),
        P(("ctx", "roll"), None),
        P(("ctx", "roll"), None),
        P(("ctx", "roll"), None),
    )
    return jax.shard_map(
        body,
        mesh=mesh,
        in_specs=placed,
        out_specs=(
            P("ctx", None),
            P("ctx", None),
            P(("ctx", "roll"), None),
            P(("ctx", "roll"), None),
            P(("ctx", "roll"), None),
            P("ctx", None),
        ),
        check_vma=False,
    )
```

```python
import functools

import jax
import jax.numpy as jnp
from jax import lax
from jax.experimental import pallas as pl
from jax.experimental.pallas import tpu as pltpu
from jax.sharding import PartitionSpec as P


NEG_FILL = -1e30
BETA_ONE = 0.9
BETA_TWO = 0.95
ADAM_EPS = 1e-08
DECAY_RATE = 0.1
LEARN_RATE = 1e-06
CORRECT_ONE = 0.9999734386011124
CORRECT_TWO = 0.994079470779666


def shifted(value, axis, count, shift):
    return lax.ppermute(value, axis, [(i, (i + shift) % count) for i in range(count)])


def attention_kernel(block_count, block_rows, head_dim, score_scale, *refs):
    order_ref, rank_ref, seg_ref, q_ref, do_ref, own_ref, mine_ref, other_ref = refs[:8]
    half = mine_ref.shape[0]
    dq_ref = refs[8]
    part_refs = refs[9 : 10 + half]
    key_scr, value_scr, mask_scr, dk_acc, dv_acc = refs[10 + half :]
    low_is_mine = rank_ref[1] == 0

    def kv_block(b, which):
        if b == 0:
            return own_ref[which]
        if b <= half:
            return jnp.where(low_is_mine, mine_ref[b - 1, which], other_ref[b - 1, which])
        return jnp.where(low_is_mine, other_ref[b - 1 - half, which], mine_ref[b - 1 - half, which])

    step = pl.program_id(0)

    @pl.when(step == 0)
    def _():
        rank = rank_ref[0]
        lane = lax.broadcasted_iota(jnp.int32, (block_rows, block_rows), 1)
        sub = lax.broadcasted_iota(jnp.int32, (block_rows, block_rows), 0)
        own_seg = seg_ref[pl.ds(rank, 1), :]
        q_seg = jnp.sum(jnp.where(lane == sub, own_seg, 0), axis=1, keepdims=True)
        q_pos = order_ref[rank] * block_rows + sub[:, :1]
        for b in range(block_count):
            source = (rank + b) % block_count
            k_pos = order_ref[source] * block_rows + lane[:1, :]
            k_seg = seg_ref[pl.ds(source, 1), :]
            visible = (k_pos <= q_pos) & (k_seg == q_seg)
            cols = slice(b * block_rows, (b + 1) * block_rows)
            mask_scr[:, cols] = visible.astype(jnp.int32)
            key_block = kv_block(b, 0)
            key_scr[cols, :] = key_block
            value_scr[cols, :] = kv_block(b, 1)
        dk_acc[...] = jnp.zeros_like(dk_acc)
        dv_acc[...] = jnp.zeros_like(dv_acc)

    head_count = q_ref.shape[1] // head_dim
    key_count = block_count * block_rows
    pair = max(
        g for g in range(1, head_count + 1)
        if head_count % g == 0 and g * q_ref.shape[0] * key_count <= 768 * 1024
    ) if q_ref.shape[0] * key_count <= 768 * 1024 else 1
    visible_rows = mask_scr[...] != 0
    visible = jnp.concatenate([visible_rows] * pair, axis=0) if pair > 1 else visible_rows
    for h in range(0, head_count, pair):
        head_cols = [slice((h + i) * head_dim, (h + i + 1) * head_dim) for i in range(pair)]
        q = jnp.concatenate([q_ref[:, c] for c in head_cols], axis=0) if pair > 1 else q_ref[:, head_cols[0]]
        do = jnp.concatenate([do_ref[:, c] for c in head_cols], axis=0) if pair > 1 else do_ref[:, head_cols[0]]
        scores = lax.dot_general(q, key_scr[...], (((1,), (1,)), ((), ())), preferred_element_type=jnp.float32) * score_scale
        scores = jnp.where(visible, scores, NEG_FILL)
        row_top = jnp.max(scores, axis=1, keepdims=True)
        expo = jnp.where(visible, jnp.exp(scores - row_top), 0.0)
        weights = expo * (1.0 / jnp.sum(expo, axis=1, keepdims=True))
        dprob = lax.dot_general(do, value_scr[...], (((1,), (1,)), ((), ())), preferred_element_type=jnp.float32)
        delta = jnp.sum(weights * dprob, axis=1, keepdims=True)
        dscore = weights * (dprob - delta)
        weights_half = weights.astype(jnp.bfloat16)
        dscore_half = dscore.astype(jnp.bfloat16)
        query_part = jnp.dot(dscore_half, key_scr[...], preferred_element_type=jnp.float32) * score_scale
        rows = query_part.shape[0] // pair
        for i, c in enumerate(head_cols):
            dq_ref[:, c] = query_part[i * rows : (i + 1) * rows].astype(dq_ref.dtype)
        q_t = q.astype(jnp.float32).T.astype(jnp.bfloat16)
        do_t = do.astype(jnp.float32).T.astype(jnp.bfloat16)
        dk_acc[...] += jnp.dot(q_t, dscore_half, preferred_element_type=jnp.float32)
        dv_acc[...] += jnp.dot(do_t, weights_half, preferred_element_type=jnp.float32)

    @pl.when(step == pl.num_programs(0) - 1)
    def _():
        def part_of(b):
            cols = slice(b * block_rows, (b + 1) * block_rows)
            key_part = (dk_acc[:, cols].T * score_scale).astype(jnp.bfloat16)
            value_part = dv_acc[:, cols].T.astype(jnp.bfloat16)
            return key_part, value_part

        own_key, own_value = part_of(0)
        part_refs[0][:, :head_dim] = own_key
        part_refs[0][:, head_dim:] = own_value
        for k in range(half):
            low_key, low_value = part_of(1 + k)
            if 1 + k + half < block_count:
                high_key, high_value = part_of(1 + k + half)
                low_key = jnp.where(low_is_mine, low_key, high_key)
                low_value = jnp.where(low_is_mine, low_value, high_value)
            part_refs[1 + k][:, :head_dim] = low_key
            part_refs[1 + k][:, head_dim:] = low_value


def attention_backward(block_order, rank, seg_rows, query_states, out_grad, own_kv, mine, other, head_dim, score_scale):
    row_count, width = query_states.shape
    head_group = width // head_dim
    block_count = seg_rows.shape[0]
    block_rows = own_kv.shape[1]
    key_count = block_count * block_rows
    full = lambda shape: pl.BlockSpec(shape, lambda h, *_: (0,) * len(shape))
    head = pl.BlockSpec((row_count, width), lambda h, *_: (0, 0))
    part = jax.ShapeDtypeStruct((block_rows, 2 * head_dim), jnp.bfloat16)
    kernel = functools.partial(attention_kernel, block_count, block_rows, head_dim, score_scale)
    outs = pl.pallas_call(
        kernel,
        grid_spec=pltpu.PrefetchScalarGridSpec(
            num_scalar_prefetch=2,
            grid=(1,),
            in_specs=[full(seg_rows.shape), head, head, full(own_kv.shape), full(mine.shape), full(other.shape)],
            out_specs=[head] + [full((block_rows, 2 * head_dim))] * (1 + mine.shape[0]),
            scratch_shapes=[
                pltpu.VMEM((key_count, head_dim), jnp.bfloat16),
                pltpu.VMEM((key_count, head_dim), jnp.bfloat16),
                pltpu.VMEM((row_count, key_count), jnp.int32),
                pltpu.VMEM((head_dim, key_count), jnp.float32),
                pltpu.VMEM((head_dim, key_count), jnp.float32),
            ],
        ),
        out_shape=[jax.ShapeDtypeStruct((row_count, width), jnp.bfloat16)] + [part] * (1 + mine.shape[0]),
        compiler_params=pltpu.CompilerParams(dimension_semantics=("arbitrary",)),
    )(block_order, rank, seg_rows, query_states, out_grad, own_kv, mine, other)
    return outs[0], outs[1:]


def middle_kernel(block_count, head_dim, *refs):
    rank_ref, roll_ref, rows_ref, own_ref, mine_ref, other_ref, kv_ref = refs[:7]
    out_refs = refs[7:]
    low_is_mine = roll_ref[0] % 2 == 0
    low = jnp.where(low_is_mine, mine_ref[...], other_ref[...])
    high = jnp.where(low_is_mine, other_ref[...], mine_ref[...])
    total = own_ref[...].astype(jnp.float32) + low + high
    key_value = total.astype(jnp.bfloat16)
    kv_ref[...] = key_value
    key_grad = key_value[:, :head_dim]
    rank = rank_ref[0]
    for s in range(block_count):
        rows = rows_ref[(rank + s) % block_count]
        out_refs[s][...] = jnp.dot(rows, key_grad, preferred_element_type=jnp.float32).astype(jnp.bfloat16)


def key_value_and_products(rank, roll_rank, layer_input, own_part, mine, other, roll_count, owner_rows):
    block_count = layer_input.shape[0] // (roll_count * owner_rows)
    row_count, width = own_part.shape
    head_dim = width // 2
    features = layer_input.reshape(block_count, roll_count, owner_rows, row_count)
    full = lambda shape: pl.BlockSpec(shape, lambda i, *_: (0,) * len(shape))
    picked = pl.BlockSpec((block_count, None, owner_rows, row_count), lambda i, rank_ref, roll_ref: (0, roll_ref[0], 0, 0))
    product = jax.ShapeDtypeStruct((owner_rows, head_dim), jnp.bfloat16)
    outs = pl.pallas_call(
        functools.partial(middle_kernel, block_count, head_dim),
        grid_spec=pltpu.PrefetchScalarGridSpec(
            num_scalar_prefetch=2,
            grid=(1,),
            in_specs=[picked] + [full((row_count, width))] * 3,
            out_specs=[full((row_count, width))] + [full((owner_rows, head_dim))] * block_count,
        ),
        out_shape=[jax.ShapeDtypeStruct((row_count, width), jnp.bfloat16)] + [product] * block_count,
    )(rank, roll_rank, features, own_part, mine, other)
    return outs[0], outs[1:]


def body(
    block_order,
    segment_ids,
    layer_input,
    query_states,
    key_states,
    value_states,
    out_grad,
    master_weight,
    first_moment,
    second_moment,
):
    row_count, head_dim = key_states.shape
    head_group = query_states.shape[1] // head_dim
    ctx_count = lax.axis_size("ctx")
    roll_count = lax.axis_size("roll")
    ctx_rank = lax.axis_index("ctx")
    roll_rank = lax.axis_index("roll")
    score_scale = head_dim ** (-0.5)

    seg_table = segment_ids.reshape(ctx_count, row_count)
    rank_vector = jnp.reshape(ctx_rank, (1,)).astype(jnp.int32)

    own_kv = jnp.stack([key_states, value_states])
    half = ctx_count // 2
    fetched = []
    for k in range(half):
        pairs = []
        for c in range(ctx_count):
            for r in range(roll_count):
                s = 1 + k + half * (r % 2)
                if s < ctx_count:
                    pairs.append((c * roll_count + r, ((c - s) % ctx_count) * roll_count + r))
        fetched.append(lax.ppermute(own_kv, ("ctx", "roll"), pairs))
    mine = jnp.stack(fetched)
    other = lax.ppermute(mine, "roll", [(r, r ^ 1) for r in range(roll_count)])
    core_rank = jnp.stack([ctx_rank, roll_rank % 2]).astype(jnp.int32)
    query_grad, part_blocks = attention_backward(
        block_order,
        core_rank,
        seg_table,
        query_states,
        out_grad,
        own_kv,
        mine,
        other,
        head_dim,
        score_scale,
    )

    mine_sum = None
    for k in range(half):
        pairs = []
        for c in range(ctx_count):
            for r in range(roll_count):
                s = 1 + k + half * (r % 2)
                if s < ctx_count:
                    pairs.append((c * roll_count + r, ((c + s) % ctx_count) * roll_count + r))
        arrived = lax.ppermute(part_blocks[1 + k], ("ctx", "roll"), pairs).astype(jnp.float32)
        mine_sum = arrived if mine_sum is None else mine_sum + arrived
    other_sum = lax.ppermute(mine_sum, "roll", [(r, r ^ 1) for r in range(roll_count)])
    owner_rows = master_weight.shape[0]
    key_value, products = key_value_and_products(
        rank_vector,
        jnp.reshape(roll_rank, (1,)).astype(jnp.int32),
        layer_input,
        part_blocks[0],
        mine_sum,
        other_sum,
        roll_count,
        owner_rows,
    )
    weight_grad = products[0].astype(jnp.float32)
    for s in range(1, ctx_count):
        weight_grad = weight_grad + shifted(products[s], "ctx", ctx_count, s).astype(jnp.float32)

    updated_first = BETA_ONE * first_moment + (1.0 - BETA_ONE) * weight_grad
    updated_second = BETA_TWO * second_moment + (1.0 - BETA_TWO) * weight_grad * weight_grad
    update = (
        updated_first / CORRECT_ONE / (jnp.sqrt(updated_second / CORRECT_TWO) + ADAM_EPS)
        + DECAY_RATE * master_weight
    )
    updated_master = master_weight - LEARN_RATE * update
    rollout_weight = lax.all_gather(updated_master.astype(jnp.bfloat16), "roll", axis=0, tiled=True)
    return (query_grad, key_value, updated_master, updated_first, updated_second, rollout_weight)


def solution(mesh):
    placed = (
        P(),
        P(),
        P(None, "ctx"),
        P("ctx", None),
        P("ctx", None),
        P("ctx", None),
        P("ctx", None),
        P(("ctx", "roll"), None),
        P(("ctx", "roll"), None),
        P(("ctx", "roll"), None),
    )
    return jax.shard_map(
        body,
        mesh=mesh,
        in_specs=placed,
        out_specs=(
            P("ctx", None),
            P("ctx", None),
            P(("ctx", "roll"), None),
            P(("ctx", "roll"), None),
            P(("ctx", "roll"), None),
            P("ctx", None),
        ),
        check_vma=False,
    )
```

```python
import functools

import jax
import jax.numpy as jnp
from jax import lax
from jax.experimental import pallas as pl
from jax.experimental.pallas import tpu as pltpu
from jax.sharding import PartitionSpec as P


NEG_FILL = -1e30
BETA_ONE = 0.9
BETA_TWO = 0.95
ADAM_EPS = 1e-08
DECAY_RATE = 0.1
LEARN_RATE = 1e-06
CORRECT_ONE = 0.9999734386011124
CORRECT_TWO = 0.994079470779666


def shifted(value, axis, count, shift):
    return lax.ppermute(value, axis, [(i, (i + shift) % count) for i in range(count)])


def attention_kernel(block_count, block_rows, head_dim, score_scale, *refs):
    order_ref, rank_ref, seg_ref, q_ref, do_ref, own_ref, mine_ref, other_ref = refs[:8]
    half = mine_ref.shape[0]
    dq_ref = refs[8]
    part_refs = refs[9 : 10 + half]
    key_scr, kt_scr, vt_scr, mask_scr, dk_acc, dv_acc = refs[10 + half :]
    low_is_mine = rank_ref[1] == 0

    def kv_block(b, which):
        if b == 0:
            return own_ref[which]
        if b <= half:
            return jnp.where(low_is_mine, mine_ref[b - 1, which], other_ref[b - 1, which])
        return jnp.where(low_is_mine, other_ref[b - 1 - half, which], mine_ref[b - 1 - half, which])

    step = pl.program_id(0)

    @pl.when(step == 0)
    def _():
        rank = rank_ref[0]
        lane = lax.broadcasted_iota(jnp.int32, (block_rows, block_rows), 1)
        sub = lax.broadcasted_iota(jnp.int32, (block_rows, block_rows), 0)
        own_seg = seg_ref[pl.ds(rank, 1), :]
        q_seg = jnp.sum(jnp.where(lane == sub, own_seg, 0), axis=1, keepdims=True)
        q_pos = order_ref[rank] * block_rows + sub[:, :1]
        for b in range(block_count):
            source = (rank + b) % block_count
            k_pos = order_ref[source] * block_rows + lane[:1, :]
            k_seg = seg_ref[pl.ds(source, 1), :]
            visible = (k_pos <= q_pos) & (k_seg == q_seg)
            cols = slice(b * block_rows, (b + 1) * block_rows)
            mask_scr[:, cols] = visible.astype(jnp.int32)
            key_block = kv_block(b, 0)
            key_scr[cols, :] = key_block
            kt_scr[:, cols] = key_block.astype(jnp.float32).T.astype(jnp.bfloat16)
            vt_scr[:, cols] = kv_block(b, 1).astype(jnp.float32).T.astype(jnp.bfloat16)
        dk_acc[...] = jnp.zeros_like(dk_acc)
        dv_acc[...] = jnp.zeros_like(dv_acc)

    head_count = q_ref.shape[1] // head_dim
    key_count = block_count * block_rows
    pair = max(
        g for g in range(1, head_count + 1)
        if head_count % g == 0 and g * q_ref.shape[0] * key_count <= 768 * 1024
    ) if q_ref.shape[0] * key_count <= 768 * 1024 else 1
    visible_rows = mask_scr[...] != 0
    visible = jnp.concatenate([visible_rows] * pair, axis=0) if pair > 1 else visible_rows
    for h in range(0, head_count, pair):
        head_cols = [slice((h + i) * head_dim, (h + i + 1) * head_dim) for i in range(pair)]
        q = jnp.concatenate([q_ref[:, c] for c in head_cols], axis=0) if pair > 1 else q_ref[:, head_cols[0]]
        do = jnp.concatenate([do_ref[:, c] for c in head_cols], axis=0) if pair > 1 else do_ref[:, head_cols[0]]
        scores = jnp.dot(q, kt_scr[...], preferred_element_type=jnp.float32) * score_scale
        scores = jnp.where(visible, scores, NEG_FILL)
        row_top = jnp.max(scores, axis=1, keepdims=True)
        expo = jnp.where(visible, jnp.exp(scores - row_top), 0.0)
        weights = expo * (1.0 / jnp.sum(expo, axis=1, keepdims=True))
        dprob = jnp.dot(do, vt_scr[...], preferred_element_type=jnp.float32)
        delta = jnp.sum(weights * dprob, axis=1, keepdims=True)
        dscore = weights * (dprob - delta)
        weights_half = weights.astype(jnp.bfloat16)
        dscore_half = dscore.astype(jnp.bfloat16)
        query_part = jnp.dot(dscore_half, key_scr[...], preferred_element_type=jnp.float32) * score_scale
        rows = query_part.shape[0] // pair
        for i, c in enumerate(head_cols):
            dq_ref[:, c] = query_part[i * rows : (i + 1) * rows].astype(dq_ref.dtype)
        q_t = q.astype(jnp.float32).T.astype(jnp.bfloat16)
        do_t = do.astype(jnp.float32).T.astype(jnp.bfloat16)
        dk_acc[...] += jnp.dot(q_t, dscore_half, preferred_element_type=jnp.float32)
        dv_acc[...] += jnp.dot(do_t, weights_half, preferred_element_type=jnp.float32)

    @pl.when(step == pl.num_programs(0) - 1)
    def _():
        def part_of(b):
            cols = slice(b * block_rows, (b + 1) * block_rows)
            key_part = (dk_acc[:, cols].T * score_scale).astype(jnp.bfloat16)
            value_part = dv_acc[:, cols].T.astype(jnp.bfloat16)
            return key_part, value_part

        own_key, own_value = part_of(0)
        part_refs[0][:, :head_dim] = own_key
        part_refs[0][:, head_dim:] = own_value
        for k in range(half):
            low_key, low_value = part_of(1 + k)
            if 1 + k + half < block_count:
                high_key, high_value = part_of(1 + k + half)
                low_key = jnp.where(low_is_mine, low_key, high_key)
                low_value = jnp.where(low_is_mine, low_value, high_value)
            part_refs[1 + k][:, :head_dim] = low_key
            part_refs[1 + k][:, head_dim:] = low_value


def attention_backward(block_order, rank, seg_rows, query_states, out_grad, own_kv, mine, other, head_dim, score_scale):
    row_count, width = query_states.shape
    head_group = width // head_dim
    block_count = seg_rows.shape[0]
    block_rows = own_kv.shape[1]
    key_count = block_count * block_rows
    full = lambda shape: pl.BlockSpec(shape, lambda h, *_: (0,) * len(shape))
    head = pl.BlockSpec((row_count, width), lambda h, *_: (0, 0))
    part = jax.ShapeDtypeStruct((block_rows, 2 * head_dim), jnp.bfloat16)
    kernel = functools.partial(attention_kernel, block_count, block_rows, head_dim, score_scale)
    outs = pl.pallas_call(
        kernel,
        grid_spec=pltpu.PrefetchScalarGridSpec(
            num_scalar_prefetch=2,
            grid=(1,),
            in_specs=[full(seg_rows.shape), head, head, full(own_kv.shape), full(mine.shape), full(other.shape)],
            out_specs=[head] + [full((block_rows, 2 * head_dim))] * (1 + mine.shape[0]),
            scratch_shapes=[
                pltpu.VMEM((key_count, head_dim), jnp.bfloat16),
                pltpu.VMEM((head_dim, key_count), jnp.bfloat16),
                pltpu.VMEM((head_dim, key_count), jnp.bfloat16),
                pltpu.VMEM((row_count, key_count), jnp.int32),
                pltpu.VMEM((head_dim, key_count), jnp.float32),
                pltpu.VMEM((head_dim, key_count), jnp.float32),
            ],
        ),
        out_shape=[jax.ShapeDtypeStruct((row_count, width), jnp.bfloat16)] + [part] * (1 + mine.shape[0]),
        compiler_params=pltpu.CompilerParams(dimension_semantics=("arbitrary",)),
    )(block_order, rank, seg_rows, query_states, out_grad, own_kv, mine, other)
    return outs[0], outs[1:]


def middle_kernel(block_count, head_dim, *refs):
    rank_ref, roll_ref, rows_ref, own_ref, mine_ref, other_ref, kv_ref = refs[:7]
    out_refs = refs[7:]
    low_is_mine = roll_ref[0] % 2 == 0
    low = jnp.where(low_is_mine, mine_ref[...], other_ref[...])
    high = jnp.where(low_is_mine, other_ref[...], mine_ref[...])
    total = own_ref[...].astype(jnp.float32) + low + high
    key_value = total.astype(jnp.bfloat16)
    kv_ref[...] = key_value
    key_grad = key_value[:, :head_dim]
    rank = rank_ref[0]
    for s in range(block_count):
        rows = rows_ref[(rank + s) % block_count]
        out_refs[s][...] = jnp.dot(rows, key_grad, preferred_element_type=jnp.float32).astype(jnp.bfloat16)


def key_value_and_products(rank, roll_rank, layer_input, own_part, mine, other, roll_count, owner_rows):
    block_count = layer_input.shape[0] // (roll_count * owner_rows)
    row_count, width = own_part.shape
    head_dim = width // 2
    features = lax.dynamic_index_in_dim(
        layer_input.reshape(block_count, roll_count, owner_rows, row_count), roll_rank[0], 1, keepdims=False
    )
    full = lambda shape: pl.BlockSpec(shape, lambda i, *_: (0,) * len(shape))
    picked = full(features.shape)
    product = jax.ShapeDtypeStruct((owner_rows, head_dim), jnp.bfloat16)
    outs = pl.pallas_call(
        functools.partial(middle_kernel, block_count, head_dim),
        grid_spec=pltpu.PrefetchScalarGridSpec(
            num_scalar_prefetch=2,
            grid=(1,),
            in_specs=[picked] + [full((row_count, width))] * 3,
            out_specs=[full((row_count, width))] + [full((owner_rows, head_dim))] * block_count,
        ),
        out_shape=[jax.ShapeDtypeStruct((row_count, width), jnp.bfloat16)] + [product] * block_count,
    )(rank, roll_rank, features, own_part, mine, other)
    return outs[0], outs[1:]


def body(
    block_order,
    segment_ids,
    layer_input,
    query_states,
    key_states,
    value_states,
    out_grad,
    master_weight,
    first_moment,
    second_moment,
):
    row_count, head_dim = key_states.shape
    head_group = query_states.shape[1] // head_dim
    ctx_count = lax.axis_size("ctx")
    roll_count = lax.axis_size("roll")
    ctx_rank = lax.axis_index("ctx")
    roll_rank = lax.axis_index("roll")
    score_scale = head_dim ** (-0.5)

    seg_table = segment_ids.reshape(ctx_count, row_count)
    rank_vector = jnp.reshape(ctx_rank, (1,)).astype(jnp.int32)

    own_kv = jnp.stack([key_states, value_states])
    half = ctx_count // 2
    fetched = []
    for k in range(half):
        pairs = []
        for c in range(ctx_count):
            for r in range(roll_count):
                s = 1 + k + half * (r % 2)
                if s < ctx_count:
                    pairs.append((c * roll_count + r, ((c - s) % ctx_count) * roll_count + r))
        fetched.append(lax.ppermute(own_kv, ("ctx", "roll"), pairs))
    mine = jnp.stack(fetched)
    other = lax.ppermute(mine, "roll", [(r, r ^ 1) for r in range(roll_count)])
    core_rank = jnp.stack([ctx_rank, roll_rank % 2]).astype(jnp.int32)
    query_grad, part_blocks = attention_backward(
        block_order,
        core_rank,
        seg_table,
        query_states,
        out_grad,
        own_kv,
        mine,
        other,
        head_dim,
        score_scale,
    )

    mine_sum = None
    for k in range(half):
        pairs = []
        for c in range(ctx_count):
            for r in range(roll_count):
                s = 1 + k + half * (r % 2)
                if s < ctx_count:
                    pairs.append((c * roll_count + r, ((c + s) % ctx_count) * roll_count + r))
        arrived = lax.ppermute(part_blocks[1 + k], ("ctx", "roll"), pairs).astype(jnp.float32)
        mine_sum = arrived if mine_sum is None else mine_sum + arrived
    other_sum = lax.ppermute(mine_sum, "roll", [(r, r ^ 1) for r in range(roll_count)])
    owner_rows = master_weight.shape[0]
    key_value, products = key_value_and_products(
        rank_vector,
        jnp.reshape(roll_rank, (1,)).astype(jnp.int32),
        layer_input,
        part_blocks[0],
        mine_sum,
        other_sum,
        roll_count,
        owner_rows,
    )
    weight_grad = products[0].astype(jnp.float32)
    for s in range(1, ctx_count):
        weight_grad = weight_grad + shifted(products[s], "ctx", ctx_count, s).astype(jnp.float32)

    updated_first = BETA_ONE * first_moment + (1.0 - BETA_ONE) * weight_grad
    updated_second = BETA_TWO * second_moment + (1.0 - BETA_TWO) * weight_grad * weight_grad
    update = (
        updated_first / CORRECT_ONE / (jnp.sqrt(updated_second / CORRECT_TWO) + ADAM_EPS)
        + DECAY_RATE * master_weight
    )
    updated_master = master_weight - LEARN_RATE * update
    rollout_weight = lax.all_gather(updated_master.astype(jnp.bfloat16), "roll", axis=0, tiled=True)
    return (query_grad, key_value, updated_master, updated_first, updated_second, rollout_weight)


def solution(mesh):
    placed = (
        P(),
        P(),
        P(None, "ctx"),
        P("ctx", None),
        P("ctx", None),
        P("ctx", None),
        P("ctx", None),
        P(("ctx", "roll"), None),
        P(("ctx", "roll"), None),
        P(("ctx", "roll"), None),
    )
    return jax.shard_map(
        body,
        mesh=mesh,
        in_specs=placed,
        out_specs=(
            P("ctx", None),
            P("ctx", None),
            P(("ctx", "roll"), None),
            P(("ctx", "roll"), None),
            P(("ctx", "roll"), None),
            P("ctx", None),
        ),
        check_vma=False,
    )
```
